256 devices in a mesh: ctx: 16 (over z, x_hi), head: 16 (over x_lo, y, core).
Axes of the slice: x: 4 (x_hi: 2, x_lo: 2; x = x_hi * 2 + x_lo), y: 4, z: 8, core: 2. Of those that a mesh axis runs over, the one named last changes fastest.
Arguments:
- queries: bfloat16 [16384, 8192], P('ctx', 'head'), may hold values from -5.5 to 5.5
- keys: bfloat16 [16384, 512], P(('ctx', 'head')), may hold values from -5.5 to 5.5
- values: bfloat16 [16384, 512], P(('ctx', 'head')), may hold values from -6 to 6
- comp_k_weight: float32 [32, 512], replicated, may hold values from -0.79549513 to 0.79549513
- comp_v_weight: float32 [32, 512], replicated, may hold values from -1 to 1
- gate_logits: float32 [3, 64, 16384], P(None, 'head', 'ctx'), may hold values from -6 to 6
- sel_tiles: int32 [64, 64], replicated, may hold values from 0 to 243, as said below
Outputs:
- attended: bfloat16 [16384, 8192], P('ctx', 'head')
The draws below stay inside these ranges and needn't reach their ends.
Inputs may be any that keep to these rules, and one draw needn't show every extreme that they name: `sel_tiles`: among the indices of the query blocks of one ctx shard (4 blocks) for one group, exactly 2 distinct tiles lie in each ctx shard up to and including their own and none in later ones; the first index of every query block names a tile among the first 4 tiles of its own ctx shard; indices may repeat within a block.
All inputs are finite; a program needn't handle non-finite values.
Results may differ from the reference program's by a relative error of at most 0.012.
Values may be sent and summed in bfloat16 or wider, within the bound.
No kernel may reach another device: no remote copies, remote signals or barrier semaphores. Data moves between devices by JAX's collectives and lax.ppermute only.
A program may use at most 64 MiB of HBM per device.

```python
import jax
import jax.numpy as jnp
from jax import lax

H = 64
G = 4
HD = 128
KERN = 32
STRIDE = 16
TILE = 64
TOPK = 16
WIN = 512
QB = 256
CAP = 2
TOKD = 1024
TOKENS = 16384
NQB = 64


def shard_pool(key):
    ctx_count = TOKENS // TOKD
    tiles_shard = TOKD // TILE
    first_tiles = QB // TILE
    far_scores = jax.random.randint(jax.random.fold_in(key, 101), (G, ctx_count, ctx_count, tiles_shard), 0, 65536) * tiles_shard + jnp.arange(tiles_shard)
    far_pick = jnp.argsort(far_scores, axis=-1)[..., :CAP]
    own_scores = jax.random.randint(jax.random.fold_in(key, 102), (G, ctx_count, first_tiles), 0, 65536) * first_tiles + jnp.arange(first_tiles)
    own_pick = jnp.argsort(own_scores, axis=-1)[..., :CAP]
    has_top = jnp.any(own_pick == first_tiles - 1, axis=-1)
    last_shard = (jnp.arange(ctx_count) == ctx_count - 1)[None, :]
    replace_top = last_shard & jnp.logical_not(has_top)
    own_pick = own_pick.at[..., CAP - 1].set(jnp.where(replace_top, first_tiles - 1, own_pick[..., CAP - 1]))
    shard_ids = jnp.arange(ctx_count)
    diagonal_mask = (shard_ids[:, None] == shard_ids[None, :])[None, :, :, None]
    offsets = jnp.where(diagonal_mask, own_pick[:, :, None, :], far_pick)
    return (shard_ids[None, None, :, None] * tiles_shard + offsets).astype(jnp.int32)


def draw_sel_tiles(key, part):
    ctx_count = TOKENS // TOKD
    pool = shard_pool(key)
    block_count = TOKD // QB
    free_slots = block_count * (TOPK - 1)
    slot_scores = jax.random.randint(jax.random.fold_in(key, 103), (G, ctx_count, free_slots), 0, 65536) * free_slots + jnp.arange(free_slots)
    slot_order = jnp.argsort(slot_scores, axis=-1)
    pool_size = CAP * (jnp.arange(ctx_count) + 1)
    entry = slot_order % pool_size[None, :, None]
    flat_pool = pool.reshape(G, ctx_count, ctx_count * CAP)
    picks = jnp.take_along_axis(flat_pool, entry, axis=-1).reshape(G, ctx_count, block_count, TOPK - 1)
    anchor = jnp.diagonal(pool[..., 0], axis1=1, axis2=2)
    leading = jnp.broadcast_to(anchor[:, :, None, None], (G, ctx_count, block_count, 1))
    chosen = jnp.concatenate([leading, picks], axis=-1)
    return chosen.transpose(1, 2, 0, 3).reshape(NQB, G * TOPK).astype(jnp.int32)


def draw_keys(key, part):
    base_key = jax.random.fold_in(key, 1)
    base = jnp.clip(jax.random.normal(base_key, (TOKENS, G, HD), jnp.float32), -4.5, 4.5)
    return base.reshape(TOKENS, G * HD).astype(jnp.bfloat16)


def draw_queries(key, part):
    base_key = jax.random.fold_in(key, 2)
    base = jnp.clip(jax.random.normal(base_key, (TOKENS, G, H // G, HD), jnp.float32), -4.5, 4.5)
    return base.reshape(TOKENS, H * HD).astype(jnp.bfloat16)


def draw_comp_k_weight(key, part):
    base_key = jax.random.fold_in(key, 3)
    return jnp.clip(jax.random.normal(base_key, (KERN, G * HD), jnp.float32), -4.5, 4.5) * KERN ** (-0.5)


def block_scale(key, extent, split, low, top_value):
    level = 1.0
    for position, blocks in split:
        steps = jax.random.uniform(jax.random.fold_in(jax.random.fold_in(key, 6), position), (blocks,), jnp.float32, low / len(split), top_value / len(split))
        level = level * jnp.repeat(jnp.exp(steps), extent[position] // blocks).reshape((-1,) + (1,) * (len(extent) - 1 - position))
    return level


def bell_draw(rng, shape, spread, reach, cuts=(), held_as=jnp.bfloat16):
    factor_of = block_scale(rng, shape, cuts, -0.22, 0.18) if cuts else 1.0
    array = jax.random.normal(rng, shape, jnp.float32) * spread * factor_of
    return jnp.minimum(jnp.maximum(array, -reach), reach).astype(held_as)


def setup_inputs(seed: int = 0) -> dict:
    key_of = jax.random.split(jax.random.key(seed), 8)
    return {
        "queries": draw_queries(jax.random.fold_in(key_of[7], 71), 0),
        "keys": draw_keys(jax.random.fold_in(key_of[7], 71), 0),
        "values": bell_draw(key_of[2], (TOKENS, G * HD), 1.0, 6.0, ((0, 256),)),
        "comp_k_weight": draw_comp_k_weight(jax.random.fold_in(key_of[7], 71), 0),
        "comp_v_weight": bell_draw(key_of[4], (KERN, G * HD), KERN ** -0.5, 1.0, (), jnp.float32),
        "gate_logits": bell_draw(key_of[5], (3, H, TOKENS), 1.5, 6.0, ((1, 16), (2, 16)), jnp.float32),
        "sel_tiles": draw_sel_tiles(jax.random.fold_in(key_of[7], 71), 0),
    }


def attend(query_block, key_block, value_block, allowed, with_sink):
    scores = jnp.einsum("qghd,gkd->ghqk", query_block.astype(jnp.float32), key_block.astype(jnp.float32)) * (HD ** -0.5)
    masked = jnp.where(allowed, scores, -jnp.inf)
    running_max = jnp.max(masked, axis=-1)
    if with_sink:
        running_max = jnp.maximum(running_max, 0.0)
    weights = jnp.where(allowed, jnp.exp(scores - running_max[..., None]), 0.0)
    denominator = jnp.sum(weights, axis=-1)
    if with_sink:
        denominator = denominator + jnp.exp(-running_max)
    output = jnp.einsum("ghqk,gkd->ghqd", weights.astype(jnp.bfloat16).astype(jnp.float32), value_block.astype(jnp.float32))
    return output / denominator[..., None]


def arrange(stacked):
    return stacked.transpose(0, 3, 1, 2, 4).reshape(TOKENS, H, HD)


def reference(queries, keys, values, comp_k_weight, comp_v_weight, gate_logits, sel_tiles):
    group_heads = H // G
    query_all = queries.reshape(TOKENS, G, group_heads, HD)
    key_all = keys.reshape(TOKENS, G, HD)
    value_all = values.reshape(TOKENS, G, HD)
    blocks_comp = TOKENS // STRIDE

    def compress(row_block, weight):
        padded = jnp.concatenate([row_block, jnp.zeros((KERN - STRIDE, G, HD), row_block.dtype)], 0)
        first_half = padded[:TOKENS].reshape(blocks_comp, STRIDE, G, HD).astype(jnp.float32)
        second_half = padded[STRIDE:STRIDE + TOKENS].reshape(blocks_comp, STRIDE, G, HD).astype(jnp.float32)
        weight = weight.reshape(KERN, G, HD)
        merged = jnp.sum(first_half * weight[None, :STRIDE], 1) + jnp.sum(second_half * weight[None, STRIDE:], 1)
        return merged.astype(jnp.bfloat16).transpose(1, 0, 2)

    comp_keys = compress(key_all, comp_k_weight)
    comp_values = compress(value_all, comp_v_weight)
    comp_end = jnp.arange(blocks_comp).astype(jnp.int32) * STRIDE + KERN - 1
    key_groups = key_all.transpose(1, 0, 2)
    value_groups = value_all.transpose(1, 0, 2)

    def compressed_block(block_index):
        query_block = lax.dynamic_slice_in_dim(query_all, block_index * QB, QB, 0)
        positions = block_index * QB + jnp.arange(QB).astype(jnp.int32)
        allowed = comp_end[None, :] <= positions[:, None]
        return attend(query_block, comp_keys, comp_values, allowed, True)

    def selected_block(block_index):
        query_block = lax.dynamic_slice_in_dim(query_all, block_index * QB, QB, 0)
        tile_ids = sel_tiles[block_index].reshape(G, TOPK).astype(jnp.int32)
        key_rows = (tile_ids[:, :, None] * TILE + jnp.arange(TILE).astype(jnp.int32)[None, None, :]).reshape(G, TOPK * TILE)
        group_ids = jnp.arange(G).astype(jnp.int32)[:, None]
        key_block = key_groups[group_ids, key_rows]
        value_block = value_groups[group_ids, key_rows]
        repeated = tile_ids[:, :, None] == tile_ids[:, None, :]
        earlier = jnp.arange(TOPK)[None, :] < jnp.arange(TOPK)[:, None]
        seen_before = jnp.any(repeated & earlier[None], axis=-1)
        keep_key = jnp.repeat(jnp.logical_not(seen_before), TILE, axis=1)
        positions = block_index * QB + jnp.arange(QB).astype(jnp.int32)
        allowed = keep_key[:, None, None, :] & (key_rows[:, None, None, :] <= positions[None, None, :, None])
        return attend(query_block, key_block, value_block, allowed, True)

    key_pad = jnp.concatenate([jnp.zeros((WIN, G, HD), key_all.dtype), key_all], 0)
    value_pad = jnp.concatenate([jnp.zeros((WIN, G, HD), value_all.dtype), value_all], 0)

    def window_block(block_index):
        row_begin = block_index * WIN
        query_block = lax.dynamic_slice_in_dim(query_all, row_begin, WIN, 0)
        key_block = lax.dynamic_slice_in_dim(key_pad, row_begin, 2 * WIN, 0).transpose(1, 0, 2)
        value_block = lax.dynamic_slice_in_dim(value_pad, row_begin, 2 * WIN, 0).transpose(1, 0, 2)
        key_pos = row_begin - WIN + jnp.arange(2 * WIN).astype(jnp.int32)
        positions = row_begin + jnp.arange(WIN).astype(jnp.int32)
        allowed = (key_pos[None, :] <= positions[:, None]) & (key_pos[None, :] > positions[:, None] - WIN) & (key_pos[None, :] >= 0)
        return attend(query_block, key_block, value_block, allowed, False)

    comp_out = arrange(lax.map(compressed_block, jnp.arange(NQB).astype(jnp.int32)))
    sel_out = arrange(lax.map(selected_block, jnp.arange(NQB).astype(jnp.int32)))
    win_out = arrange(lax.map(window_block, jnp.arange(TOKENS // WIN).astype(jnp.int32)))
    gate_values = jax.nn.sigmoid(gate_logits).transpose(0, 2, 1)
    combined = gate_values[0][..., None] * comp_out + gate_values[1][..., None] * sel_out + gate_values[2][..., None] * win_out
    return combined.reshape(TOKENS, H * HD).astype(jnp.bfloat16)
```

```python
import functools

import jax
import jax.numpy as jnp
from jax import lax
from jax.experimental import pallas as pl
from jax.experimental.pallas import tpu as pltpu
from jax.sharding import PartitionSpec as P

H = 64
G = 4
HD = 128
KERN = 32
STRIDE = 16
TILE = 64
TOPK = 16
WIN = 512
QB = 256
CAP = 2
BIG = 1 << 30


def shifted(block, axis, distance):
    devices = range(lax.axis_size(axis))
    route = [(i - distance, i) for i in devices if i - distance in devices]
    return lax.ppermute(block, axis, route)


def branch_kernel(q_ref, kv_ref, lo_ref, hi_ref, t_ref, g_ref, *rest, sink, key_rows, row_step, heads):
    if len(rest) == 2:
        acc_ref, o_ref = rest
    else:
        acc_ref = None
        (o_ref,) = rest
    block = pl.program_id(0)
    if row_step:
        start = pl.multiple_of(block * row_step, row_step)
        kv = kv_ref[pl.ds(start, key_rows), :]
    else:
        kv = kv_ref[...]
    keys = kv[:, :HD]
    vals = kv[:, HD:]
    lo = lo_ref[0]
    hi = hi_ref[0]
    t = t_ref[...]
    allowed = (lo <= t) & (t < hi)
    for h in range(heads):
        q = q_ref[:, h * HD : (h + 1) * HD]
        s = lax.dot_general(
            q, keys, (((1,), (1,)), ((), ())), preferred_element_type=jnp.float32
        ) * HD ** (-0.5)
        m = jnp.max(jnp.where(allowed, s, -jnp.inf), axis=1, keepdims=True)
        if sink:
            m = jnp.maximum(m, 0.0)
        p = jnp.where(allowed, jnp.exp(s - m), 0.0)
        l = jnp.sum(p, axis=1, keepdims=True)
        if sink:
            l = l + jnp.exp(-m)
        o = jnp.dot(p.astype(jnp.bfloat16), vals, preferred_element_type=jnp.float32) / l
        r = g_ref[:, h : h + 1] * o
        if acc_ref is not None:
            r = acc_ref[:, h * HD : (h + 1) * HD] + r
        o_ref[:, h * HD : (h + 1) * HD] = r.astype(o_ref.dtype)


def branch(q, kv, lo, hi, t, gate, acc, *, sink, key_rows, row_step, out_dtype):
    rows, width = q.shape
    heads = width // HD
    blocks = rows // QB
    lo_map = (lambda i: (i, 0, 0)) if lo.shape[0] > 1 else (lambda i: (0, 0, 0))
    hi_map = (lambda i: (i, 0, 0)) if hi.shape[0] > 1 else (lambda i: (0, 0, 0))
    in_specs = [
        pl.BlockSpec((QB, width), lambda i: (i, 0)),
        pl.BlockSpec(kv.shape, lambda i: (0, 0)),
        pl.BlockSpec((1,) + lo.shape[1:], lo_map),
        pl.BlockSpec((1,) + hi.shape[1:], hi_map),
        pl.BlockSpec((QB, 1), lambda i: (i, 0)),
        pl.BlockSpec((QB, gate.shape[1]), lambda i: (i, 0)),
    ]
    args = [q, kv, lo, hi, t, gate]
    aliases = {}
    if acc is not None:
        in_specs.append(pl.BlockSpec((QB, width), lambda i: (i, 0)))
        args.append(acc)
        if acc.dtype == out_dtype:
            aliases = {len(args) - 1: 0}
    kernel = functools.partial(
        branch_kernel, sink=sink, key_rows=key_rows, row_step=row_step, heads=heads
    )
    flops = 4 * rows * heads * key_rows * HD
    cost = pl.CostEstimate(
        flops=flops,
        transcendentals=rows * heads * key_rows,
        bytes_accessed=q.size * 2 + kv.size * 2 + rows * width * 8,
    )
    return pl.pallas_call(
        kernel,
        grid=(blocks,),
        in_specs=in_specs,
        out_specs=pl.BlockSpec((QB, width), lambda i: (i, 0)),
        out_shape=jax.ShapeDtypeStruct((rows, width), out_dtype),
        input_output_aliases=aliases,
        compiler_params=pltpu.CompilerParams(
            dimension_semantics=("arbitrary",), vmem_limit_bytes=48 * 1024 * 1024
        ),
        cost_estimate=cost,
    )(*args)


def local(queries, keys, values, comp_k_weight, comp_v_weight, gate_logits, sel_tiles):
    ctx_count = lax.axis_size("ctx")
    head_count = lax.axis_size("head")
    ctx_index = lax.axis_index("ctx")
    head_index = lax.axis_index("head")
    local_rows = queries.shape[0]
    local_heads = queries.shape[1] // HD
    group_index = head_index * local_heads // (H // G)
    dev_rows = keys.shape[0]
    kv_rows = jnp.concatenate(
        [keys.reshape(dev_rows, G, HD), values.reshape(dev_rows, G, HD)], axis=2
    ).transpose(1, 0, 2)
    dest_group = jnp.arange(head_count) * local_heads // (H // G)
    outbox_kv = kv_rows[dest_group]
    group_kv = lax.all_to_all(outbox_kv, "head", 0, 0, tiled=True).reshape(
        local_rows, 2 * HD
    )
    tail_rows = shifted(group_kv[: KERN - STRIDE], "ctx", -1)
    extended = jnp.concatenate([group_kv, tail_rows], axis=0)
    comp_weight = jnp.concatenate(
        [
            lax.dynamic_slice_in_dim(comp_k_weight, group_index * HD, HD, 1),
            lax.dynamic_slice_in_dim(comp_v_weight, group_index * HD, HD, 1),
        ],
        axis=1,
    )
    comp_local = local_rows // STRIDE
    first_half = extended[:local_rows].reshape(comp_local, STRIDE, 2 * HD).astype(jnp.float32)
    second_half = (
        extended[STRIDE : STRIDE + local_rows]
        .reshape(comp_local, STRIDE, 2 * HD)
        .astype(jnp.float32)
    )
    compressed = (
        jnp.sum(first_half * comp_weight[None, :STRIDE], 1)
        + jnp.sum(second_half * comp_weight[None, STRIDE:], 1)
    ).astype(jnp.bfloat16)
    comp_kv = lax.all_gather(compressed, "ctx", axis=0, tiled=True)
    comp_count = comp_kv.shape[0]
    previous = shifted(group_kv[local_rows - WIN :], "ctx", 1)
    window_kv = jnp.concatenate([previous, group_kv], axis=0)

    block_count = local_rows // QB
    tiles_shard = local_rows // TILE
    group_tiles = lax.dynamic_slice_in_dim(sel_tiles, group_index * TOPK, TOPK, 1)
    own_tiles = lax.dynamic_slice_in_dim(group_tiles, ctx_index * block_count, block_count, 0)
    own_flat = own_tiles.reshape(-1)
    requests = group_tiles.reshape(ctx_count, block_count * TOPK)
    local_ids = ctx_index * tiles_shard + jnp.arange(tiles_shard)
    present = jnp.any(requests[:, :, None] == local_ids[None, None, :], axis=1)
    order_rank = jnp.cumsum(present.astype(jnp.int32), axis=1) - 1
    picked = present[:, None, :] & (order_rank[:, None, :] == jnp.arange(CAP)[None, :, None])
    outbox = jnp.einsum(
        "dct,tx->dcx",
        picked.astype(jnp.bfloat16),
        group_kv.reshape(tiles_shard, TILE * 2 * HD),
        preferred_element_type=jnp.float32,
    ).astype(jnp.bfloat16)
    received = lax.all_to_all(outbox, "ctx", split_axis=0, concat_axis=0, tiled=True)
    all_ids = jnp.arange(ctx_count * tiles_shard).reshape(ctx_count, tiles_shard)
    wanted = jnp.any(own_flat[:, None, None] == all_ids[None, :, :], axis=0)
    wanted_rank = jnp.cumsum(wanted.astype(jnp.int32), axis=1) - 1
    chosen = wanted[:, None, :] & (wanted_rank[:, None, :] == jnp.arange(CAP)[None, :, None])
    slot_tile = jnp.sum(jnp.where(chosen, all_ids[:, None, :], 0), axis=2).reshape(-1)
    slot_ok = jnp.any(chosen, axis=2).reshape(-1)
    sel_kv = received.reshape(ctx_count * CAP * TILE, 2 * HD)
    sel_rows = sel_kv.shape[0]
    key_pos = (slot_tile[:, None] * TILE + jnp.arange(TILE)[None, :]).reshape(-1)
    is_named = slot_ok[None, :] & jnp.any(
        own_tiles[:, :, None] == slot_tile[None, None, :], axis=1
    )
    sel_lo = jnp.where(jnp.repeat(is_named, TILE, axis=1), key_pos[None, :], BIG).reshape(
        block_count, 1, sel_rows
    )
    never = jnp.full((1, 1, sel_rows), BIG, jnp.int32)

    comp_lo = (jnp.arange(comp_count, dtype=jnp.int32) * STRIDE + KERN - 1).reshape(
        1, 1, comp_count
    )
    comp_hi = jnp.full((1, 1, comp_count), BIG, jnp.int32)

    win_rows = QB + WIN
    win_pos = (
        ctx_index * local_rows
        - WIN
        + jnp.arange(block_count)[:, None] * QB
        + jnp.arange(win_rows)[None, :]
    )
    win_lo = jnp.where(win_pos >= 0, win_pos, BIG).reshape(block_count, 1, win_rows)
    win_hi = (win_pos + WIN).reshape(block_count, 1, win_rows)

    positions = (ctx_index * local_rows + jnp.arange(local_rows, dtype=jnp.int32)).reshape(
        local_rows, 1
    )
    gate_values = jax.nn.sigmoid(gate_logits).transpose(0, 2, 1)

    acc = branch(
        queries, window_kv, win_lo, win_hi, positions, gate_values[2], None,
        sink=False, key_rows=win_rows, row_step=QB, out_dtype=jnp.float32,
    )
    acc = branch(
        queries, comp_kv, comp_lo, comp_hi, positions, gate_values[0], acc,
        sink=True, key_rows=comp_count, row_step=0, out_dtype=jnp.float32,
    )
    return branch(
        queries, sel_kv, sel_lo, never, positions, gate_values[1], acc,
        sink=True, key_rows=sel_rows, row_step=0, out_dtype=jnp.bfloat16,
    )


def solution(mesh):
    placed = (
        P("ctx", "head"),
        P(("ctx", "head"), None),
        P(("ctx", "head"), None),
        P(),
        P(),
        P(None, "head", "ctx"),
        P(),
    )
    return jax.shard_map(
        local, mesh=mesh, in_specs=placed, out_specs=P("ctx", "head"), check_vma=False
    )
```

```python
import functools

import jax
import jax.numpy as jnp
from jax import lax
from jax.experimental import pallas as pl
from jax.experimental.pallas import tpu as pltpu
from jax.sharding import PartitionSpec as P

H = 64
G = 4
HD = 128
KERN = 32
STRIDE = 16
TILE = 64
TOPK = 16
WIN = 512
QB = 256
CAP = 2
BIG = 1 << 30


def shifted(block, axis, distance):
    devices = range(lax.axis_size(axis))
    route = [(i - distance, i) for i in devices if i - distance in devices]
    return lax.ppermute(block, axis, route)


def branch_kernel(q_ref, kv_ref, lo_ref, hi_ref, t_ref, g_ref, *rest, sink, key_rows, row_step, heads):
    if len(rest) == 2:
        acc_ref, o_ref = rest
    else:
        acc_ref = None
        (o_ref,) = rest
    block = pl.program_id(0)
    if row_step:
        start = pl.multiple_of(block * row_step, row_step)
        kv = kv_ref[pl.ds(start, key_rows), :]
    else:
        kv = kv_ref[...]
    keys = kv[:, :HD]
    vals = kv[:, HD:]
    lo = lo_ref[0]
    hi = hi_ref[0]
    t = t_ref[...]
    bias = jnp.where((lo <= t) & (t < hi), 0.0, -jnp.inf)
    for h in range(heads):
        q = q_ref[:, h * HD : (h + 1) * HD]
        s = lax.dot_general(
            q, keys, (((1,), (1,)), ((), ())), preferred_element_type=jnp.float32
        ) * HD ** (-0.5) + bias
        m = jnp.max(s, axis=1, keepdims=True)
        if sink:
            m = jnp.maximum(m, 0.0)
        p = jnp.exp(s - m)
        l = jnp.sum(p, axis=1, keepdims=True)
        if sink:
            l = l + jnp.exp(-m)
        o = jnp.dot(p.astype(jnp.bfloat16), vals, preferred_element_type=jnp.float32) / l
        r = g_ref[:, h : h + 1] * o
        if acc_ref is not None:
            r = acc_ref[:, h * HD : (h + 1) * HD] + r
        o_ref[:, h * HD : (h + 1) * HD] = r.astype(o_ref.dtype)


def branch(q, kv, lo, hi, t, gate, acc, *, sink, key_rows, row_step, out_dtype):
    rows, width = q.shape
    heads = width // HD
    blocks = rows // QB
    lo_map = (lambda i: (i, 0, 0)) if lo.shape[0] > 1 else (lambda i: (0, 0, 0))
    hi_map = (lambda i: (i, 0, 0)) if hi.shape[0] > 1 else (lambda i: (0, 0, 0))
    in_specs = [
        pl.BlockSpec((QB, width), lambda i: (i, 0)),
        pl.BlockSpec(kv.shape, lambda i: (0, 0)),
        pl.BlockSpec((1,) + lo.shape[1:], lo_map),
        pl.BlockSpec((1,) + hi.shape[1:], hi_map),
        pl.BlockSpec((QB, 1), lambda i: (i, 0)),
        pl.BlockSpec((QB, gate.shape[1]), lambda i: (i, 0)),
    ]
    args = [q, kv, lo, hi, t, gate]
    aliases = {}
    if acc is not None:
        in_specs.append(pl.BlockSpec((QB, width), lambda i: (i, 0)))
        args.append(acc)
        if acc.dtype == out_dtype:
            aliases = {len(args) - 1: 0}
    kernel = functools.partial(
        branch_kernel, sink=sink, key_rows=key_rows, row_step=row_step, heads=heads
    )
    flops = 4 * rows * heads * key_rows * HD
    cost = pl.CostEstimate(
        flops=flops,
        transcendentals=rows * heads * key_rows,
        bytes_accessed=q.size * 2 + kv.size * 2 + rows * width * 8,
    )
    return pl.pallas_call(
        kernel,
        grid=(blocks,),
        in_specs=in_specs,
        out_specs=pl.BlockSpec((QB, width), lambda i: (i, 0)),
        out_shape=jax.ShapeDtypeStruct((rows, width), out_dtype),
        input_output_aliases=aliases,
        compiler_params=pltpu.CompilerParams(
            dimension_semantics=("arbitrary",), vmem_limit_bytes=48 * 1024 * 1024
        ),
        cost_estimate=cost,
    )(*args)


def local(queries, keys, values, comp_k_weight, comp_v_weight, gate_logits, sel_tiles):
    ctx_count = lax.axis_size("ctx")
    head_count = lax.axis_size("head")
    ctx_index = lax.axis_index("ctx")
    head_index = lax.axis_index("head")
    local_rows = queries.shape[0]
    local_heads = queries.shape[1] // HD
    group_index = head_index * local_heads // (H // G)
    dev_rows = keys.shape[0]
    kv_rows = jnp.concatenate(
        [keys.reshape(dev_rows, G, HD), values.reshape(dev_rows, G, HD)], axis=2
    ).transpose(1, 0, 2)
    dest_group = jnp.arange(head_count) * local_heads // (H // G)
    outbox_kv = kv_rows[dest_group]
    group_kv = lax.all_to_all(outbox_kv, "head", 0, 0, tiled=True).reshape(
        local_rows, 2 * HD
    )
    tail_rows = shifted(group_kv[: KERN - STRIDE], "ctx", -1)
    extended = jnp.concatenate([group_kv, tail_rows], axis=0)
    comp_weight = jnp.concatenate(
        [
            lax.dynamic_slice_in_dim(comp_k_weight, group_index * HD, HD, 1),
            lax.dynamic_slice_in_dim(comp_v_weight, group_index * HD, HD, 1),
        ],
        axis=1,
    )
    comp_local = local_rows // STRIDE
    first_half = extended[:local_rows].reshape(comp_local, STRIDE, 2 * HD).astype(jnp.float32)
    second_half = (
        extended[STRIDE : STRIDE + local_rows]
        .reshape(comp_local, STRIDE, 2 * HD)
        .astype(jnp.float32)
    )
    compressed = (
        jnp.sum(first_half * comp_weight[None, :STRIDE], 1)
        + jnp.sum(second_half * comp_weight[None, STRIDE:], 1)
    ).astype(jnp.bfloat16)
    previous = shifted(group_kv[local_rows - WIN :], "ctx", 1)
    window_kv = jnp.concatenate([previous, group_kv], axis=0)

    block_count = local_rows // QB
    tiles_shard = local_rows // TILE
    group_tiles = lax.dynamic_slice_in_dim(sel_tiles, group_index * TOPK, TOPK, 1)
    own_tiles = lax.dynamic_slice_in_dim(group_tiles, ctx_index * block_count, block_count, 0)
    own_flat = own_tiles.reshape(-1)
    requests = group_tiles.reshape(ctx_count, block_count * TOPK)
    local_ids = ctx_index * tiles_shard + jnp.arange(tiles_shard)
    present = jnp.any(requests[:, :, None] == local_ids[None, None, :], axis=1)
    order_rank = jnp.cumsum(present.astype(jnp.int32), axis=1) - 1
    picked = present[:, None, :] & (order_rank[:, None, :] == jnp.arange(CAP)[None, :, None])
    outbox = jnp.einsum(
        "dct,tx->dcx",
        picked.astype(jnp.bfloat16),
        group_kv.reshape(tiles_shard, TILE * 2 * HD),
        preferred_element_type=jnp.float32,
    ).astype(jnp.bfloat16)
    comp_slot = jnp.broadcast_to(
        compressed.reshape(1, 1, comp_local * 2 * HD), (ctx_count, 1, comp_local * 2 * HD)
    )
    mail = jnp.concatenate([outbox, comp_slot], axis=1)
    arrived = lax.all_to_all(mail, "ctx", split_axis=0, concat_axis=0, tiled=True)
    received = arrived[:, :CAP]
    comp_kv = arrived[:, CAP].reshape(ctx_count * comp_local, 2 * HD)
    comp_count = comp_kv.shape[0]
    all_ids = jnp.arange(ctx_count * tiles_shard).reshape(ctx_count, tiles_shard)
    wanted = jnp.any(own_flat[:, None, None] == all_ids[None, :, :], axis=0)
    wanted_rank = jnp.cumsum(wanted.astype(jnp.int32), axis=1) - 1
    chosen = wanted[:, None, :] & (wanted_rank[:, None, :] == jnp.arange(CAP)[None, :, None])
    slot_tile = jnp.sum(jnp.where(chosen, all_ids[:, None, :], 0), axis=2).reshape(-1)
    slot_ok = jnp.any(chosen, axis=2).reshape(-1)
    sel_kv = received.reshape(ctx_count * CAP * TILE, 2 * HD)
    sel_rows = sel_kv.shape[0]
    key_pos = (slot_tile[:, None] * TILE + jnp.arange(TILE)[None, :]).reshape(-1)
    is_named = slot_ok[None, :] & jnp.any(
        own_tiles[:, :, None] == slot_tile[None, None, :], axis=1
    )
    sel_lo = jnp.where(jnp.repeat(is_named, TILE, axis=1), key_pos[None, :], BIG).reshape(
        block_count, 1, sel_rows
    )
    never = jnp.full((1, 1, sel_rows), BIG, jnp.int32)

    comp_lo = (jnp.arange(comp_count, dtype=jnp.int32) * STRIDE + KERN - 1).reshape(
        1, 1, comp_count
    )
    comp_hi = jnp.full((1, 1, comp_count), BIG, jnp.int32)

    win_rows = QB + WIN
    win_pos = (
        ctx_index * local_rows
        - WIN
        + jnp.arange(block_count)[:, None] * QB
        + jnp.arange(win_rows)[None, :]
    )
    win_lo = jnp.where(win_pos >= 0, win_pos, BIG).reshape(block_count, 1, win_rows)
    win_hi = (win_pos + WIN).reshape(block_count, 1, win_rows)

    positions = (ctx_index * local_rows + jnp.arange(local_rows, dtype=jnp.int32)).reshape(
        local_rows, 1
    )
    gate_values = jax.nn.sigmoid(gate_logits).transpose(0, 2, 1)

    acc = branch(
        queries, window_kv, win_lo, win_hi, positions, gate_values[2], None,
        sink=False, key_rows=win_rows, row_step=QB, out_dtype=jnp.float32,
    )
    acc = branch(
        queries, comp_kv, comp_lo, comp_hi, positions, gate_values[0], acc,
        sink=True, key_rows=comp_count, row_step=0, out_dtype=jnp.float32,
    )
    return branch(
        queries, sel_kv, sel_lo, never, positions, gate_values[1], acc,
        sink=True, key_rows=sel_rows, row_step=0, out_dtype=jnp.bfloat16,
    )


def solution(mesh):
    placed = (
        P("ctx", "head"),
        P(("ctx", "head"), None),
        P(("ctx", "head"), None),
        P(),
        P(),
        P(None, "head", "ctx"),
        P(),
    )
    return jax.shard_map(
        local, mesh=mesh, in_specs=placed, out_specs=P("ctx", "head"), check_vma=False
    )
```

```python
import functools

import jax
import jax.numpy as jnp
from jax import lax
from jax.experimental import pallas as pl
from jax.experimental.pallas import tpu as pltpu
from jax.sharding import PartitionSpec as P

H = 64
G = 4
HD = 128
KERN = 32
STRIDE = 16
TILE = 64
TOPK = 16
WIN = 512
QB = 256
CAP = 2
BIG = 1 << 30


def shifted(block, axis, distance):
    devices = range(lax.axis_size(axis))
    route = [(i - distance, i) for i in devices if i - distance in devices]
    return lax.ppermute(block, axis, route)


def branch_kernel(q_ref, kv_ref, lo_ref, hi_ref, t_ref, g_ref, *rest, sink, key_rows, row_step, heads):
    if len(rest) == 2:
        acc_ref, o_ref = rest
    else:
        acc_ref = None
        (o_ref,) = rest
    block = pl.program_id(0)
    if row_step:
        start = pl.multiple_of(block * row_step, row_step)
        kv = kv_ref[pl.ds(start, key_rows), :]
    else:
        kv = kv_ref[...]
    keys = kv[:, :HD]
    vals = kv[:, HD:]
    lo = lo_ref[0]
    hi = hi_ref[0]
    t = t_ref[...]
    bias = jnp.where((lo <= t) & (t < hi), 0.0, -jnp.inf)
    for h in range(heads):
        q = q_ref[:, h * HD : (h + 1) * HD]
        s = lax.dot_general(
            q, keys, (((1,), (1,)), ((), ())), preferred_element_type=jnp.float32
        ) * HD ** (-0.5) + bias
        m = jnp.max(s, axis=1, keepdims=True)
        if sink:
            m = jnp.maximum(m, 0.0)
        p = jnp.exp(s - m)
        l = jnp.sum(p, axis=1, keepdims=True)
        if sink:
            l = l + jnp.exp(-m)
        o = jnp.dot(p.astype(jnp.bfloat16), vals, preferred_element_type=jnp.float32) / l
        r = g_ref[:, h : h + 1] * o
        if acc_ref is not None:
            r = acc_ref[:, h * HD : (h + 1) * HD] + r
        o_ref[:, h * HD : (h + 1) * HD] = r.astype(o_ref.dtype)


def branch(q, kv, lo, hi, t, gate, acc, *, sink, key_rows, row_step, out_dtype):
    rows, width = q.shape
    heads = width // HD
    blocks = rows // QB
    lo_map = (lambda i: (i, 0, 0)) if lo.shape[0] > 1 else (lambda i: (0, 0, 0))
    hi_map = (lambda i: (i, 0, 0)) if hi.shape[0] > 1 else (lambda i: (0, 0, 0))
    in_specs = [
        pl.BlockSpec((QB, width), lambda i: (i, 0)),
        pl.BlockSpec(kv.shape, lambda i: (0, 0)),
        pl.BlockSpec((1,) + lo.shape[1:], lo_map),
        pl.BlockSpec((1,) + hi.shape[1:], hi_map),
        pl.BlockSpec((QB, 1), lambda i: (i, 0)),
        pl.BlockSpec((QB, gate.shape[1]), lambda i: (i, 0)),
    ]
    args = [q, kv, lo, hi, t, gate]
    aliases = {}
    if acc is not None:
        in_specs.append(pl.BlockSpec((QB, width), lambda i: (i, 0)))
        args.append(acc)
        if acc.dtype == out_dtype:
            aliases = {len(args) - 1: 0}
    kernel = functools.partial(
        branch_kernel, sink=sink, key_rows=key_rows, row_step=row_step, heads=heads
    )
    flops = 4 * rows * heads * key_rows * HD
    cost = pl.CostEstimate(
        flops=flops,
        transcendentals=rows * heads * key_rows,
        bytes_accessed=q.size * 2 + kv.size * 2 + rows * width * 8,
    )
    return pl.pallas_call(
        kernel,
        grid=(blocks,),
        in_specs=in_specs,
        out_specs=pl.BlockSpec((QB, width), lambda i: (i, 0)),
        out_shape=jax.ShapeDtypeStruct((rows, width), out_dtype),
        input_output_aliases=aliases,
        compiler_params=pltpu.CompilerParams(
            dimension_semantics=("arbitrary",), vmem_limit_bytes=48 * 1024 * 1024
        ),
        cost_estimate=cost,
    )(*args)


def local(queries, keys, values, comp_k_weight, comp_v_weight, gate_logits, sel_tiles):
    ctx_count = lax.axis_size("ctx")
    head_count = lax.axis_size("head")
    ctx_index = lax.axis_index("ctx")
    head_index = lax.axis_index("head")
    local_rows = queries.shape[0]
    local_heads = queries.shape[1] // HD
    group_index = head_index * local_heads // (H // G)
    dev_rows = keys.shape[0]
    kv_rows = jnp.concatenate(
        [keys.reshape(dev_rows, G, HD), values.reshape(dev_rows, G, HD)], axis=2
    ).transpose(1, 0, 2)
    dest_group = jnp.arange(head_count) * local_heads // (H // G)
    outbox_kv = kv_rows[dest_group]
    group_kv = lax.all_to_all(outbox_kv, "head", 0, 0, tiled=True).reshape(
        local_rows, 2 * HD
    )
    tail_rows = shifted(group_kv[: KERN - STRIDE], "ctx", -1)
    extended = jnp.concatenate([group_kv, tail_rows], axis=0)
    comp_weight = jnp.concatenate(
        [
            lax.dynamic_slice_in_dim(comp_k_weight, group_index * HD, HD, 1),
            lax.dynamic_slice_in_dim(comp_v_weight, group_index * HD, HD, 1),
        ],
        axis=1,
    )
    comp_local = local_rows // STRIDE
    first_half = extended[:local_rows].reshape(comp_local, STRIDE, 2 * HD).astype(jnp.float32)
    second_half = (
        extended[STRIDE : STRIDE + local_rows]
        .reshape(comp_local, STRIDE, 2 * HD)
        .astype(jnp.float32)
    )
    compressed = (
        jnp.sum(first_half * comp_weight[None, :STRIDE], 1)
        + jnp.sum(second_half * comp_weight[None, STRIDE:], 1)
    ).astype(jnp.bfloat16)
    previous = shifted(group_kv[local_rows - WIN :], "ctx", 1)
    window_kv = jnp.concatenate([previous, group_kv], axis=0)

    block_count = local_rows // QB
    tiles_shard = local_rows // TILE
    share = (H // G) // local_heads
    part = head_index % share
    groups = [[g * share + i for i in range(share)] for g in range(head_count // share)]
    sel_share = CAP * TILE // share
    comp_share = comp_local // share
    group_tiles = lax.dynamic_slice_in_dim(sel_tiles, group_index * TOPK, TOPK, 1)
    own_tiles = lax.dynamic_slice_in_dim(group_tiles, ctx_index * block_count, block_count, 0)
    own_flat = own_tiles.reshape(-1)
    requests = group_tiles.reshape(ctx_count, block_count * TOPK)
    local_ids = ctx_index * tiles_shard + jnp.arange(tiles_shard)
    present = jnp.any(requests[:, :, None] == local_ids[None, None, :], axis=1)
    order_rank = jnp.cumsum(present.astype(jnp.int32), axis=1) - 1
    my_slot = part * sel_share // TILE
    my_row = part * sel_share % TILE
    picked = present & (order_rank == my_slot)
    tile_rows = lax.dynamic_slice_in_dim(
        group_kv.reshape(tiles_shard, TILE, 2 * HD), my_row, sel_share, 1
    )
    sel_part = jnp.einsum(
        "dt,tx->dx",
        picked.astype(jnp.bfloat16),
        tile_rows.reshape(tiles_shard, sel_share * 2 * HD),
        preferred_element_type=jnp.float32,
    ).astype(jnp.bfloat16).reshape(ctx_count, sel_share, 2 * HD)
    comp_part = jnp.broadcast_to(
        lax.dynamic_slice_in_dim(compressed, part * comp_share, comp_share, 0)[None],
        (ctx_count, comp_share, 2 * HD),
    )
    mail = jnp.concatenate([sel_part, comp_part], axis=1)
    arrived = lax.all_to_all(mail, "ctx", split_axis=0, concat_axis=0, tiled=True)
    gathered = lax.all_gather(arrived, "head", axis=0, axis_index_groups=groups)
    sel_kv = gathered[:, :, :sel_share].reshape(share * ctx_count * sel_share, 2 * HD)
    comp_kv = gathered[:, :, sel_share:].reshape(share * ctx_count * comp_share, 2 * HD)
    sel_rows = sel_kv.shape[0]
    comp_count = comp_kv.shape[0]
    all_ids = jnp.arange(ctx_count * tiles_shard).reshape(ctx_count, tiles_shard)
    wanted = jnp.any(own_flat[:, None, None] == all_ids[None, :, :], axis=0)
    wanted_rank = jnp.cumsum(wanted.astype(jnp.int32), axis=1) - 1
    chosen = wanted[:, None, :] & (wanted_rank[:, None, :] == jnp.arange(CAP)[None, :, None])
    slot_tile = jnp.sum(jnp.where(chosen, all_ids[:, None, :], 0), axis=2)
    slot_ok = jnp.any(chosen, axis=2)
    payload_row = jnp.arange(share)[:, None, None] * sel_share + jnp.arange(sel_share)[None, None, :]
    source = jnp.arange(ctx_count)[None, :, None]
    key_slot = payload_row // TILE + 0 * source
    key_tile = slot_tile[source, key_slot]
    key_pos = (key_tile * TILE + payload_row % TILE).reshape(-1)
    is_named = slot_ok[None] & jnp.any(
        own_tiles[:, :, None, None] == slot_tile[None, None], axis=1
    )
    key_named = is_named[:, source, key_slot].reshape(block_count, -1)
    sel_lo = jnp.where(key_named, key_pos[None, :], BIG).reshape(block_count, 1, sel_rows)
    never = jnp.full((1, 1, sel_rows), BIG, jnp.int32)

    comp_index = (
        jnp.arange(ctx_count)[None, :, None] * comp_local
        + jnp.arange(share)[:, None, None] * comp_share
        + jnp.arange(comp_share)[None, None, :]
    ).reshape(-1)
    comp_lo = (comp_index * STRIDE + KERN - 1).astype(jnp.int32).reshape(1, 1, comp_count)
    comp_hi = jnp.full((1, 1, comp_count), BIG, jnp.int32)

    win_rows = QB + WIN
    win_pos = (
        ctx_index * local_rows
        - WIN
        + jnp.arange(block_count)[:, None] * QB
        + jnp.arange(win_rows)[None, :]
    )
    win_lo = jnp.where(win_pos >= 0, win_pos, BIG).reshape(block_count, 1, win_rows)
    win_hi = (win_pos + WIN).reshape(block_count, 1, win_rows)

    positions = (ctx_index * local_rows + jnp.arange(local_rows, dtype=jnp.int32)).reshape(
        local_rows, 1
    )
    gate_values = jax.nn.sigmoid(gate_logits).transpose(0, 2, 1)

    acc = branch(
        queries, window_kv, win_lo, win_hi, positions, gate_values[2], None,
        sink=False, key_rows=win_rows, row_step=QB, out_dtype=jnp.float32,
    )
    acc = branch(
        queries, comp_kv, comp_lo, comp_hi, positions, gate_values[0], acc,
        sink=True, key_rows=comp_count, row_step=0, out_dtype=jnp.float32,
    )
    return branch(
        queries, sel_kv, sel_lo, never, positions, gate_values[1], acc,
        sink=True, key_rows=sel_rows, row_step=0, out_dtype=jnp.bfloat16,
    )


def solution(mesh):
    placed = (
        P("ctx", "head"),
        P(("ctx", "head"), None),
        P(("ctx", "head"), None),
        P(),
        P(),
        P(None, "head", "ctx"),
        P(),
    )
    return jax.shard_map(
        local, mesh=mesh, in_specs=placed, out_specs=P("ctx", "head"), check_vma=False
    )
```

```python
import functools

import jax
import jax.numpy as jnp
from jax import lax
from jax.experimental import pallas as pl
from jax.experimental.pallas import tpu as pltpu
from jax.sharding import PartitionSpec as P

H = 64
G = 4
HD = 128
KERN = 32
STRIDE = 16
TILE = 64
TOPK = 16
WIN = 512
QB = 256
CAP = 2
BIG = 1 << 30


def shifted(block, axis, distance):
    devices = range(lax.axis_size(axis))
    route = [(i - distance, i) for i in devices if i - distance in devices]
    return lax.ppermute(block, axis, route)


def branch_kernel(q_ref, kv_ref, lo_ref, hi_ref, t_ref, g_ref, *rest, sink, key_rows, row_step, heads):
    if len(rest) == 2:
        acc_ref, o_ref = rest
    else:
        acc_ref = None
        (o_ref,) = rest
    block = pl.program_id(0)
    if row_step:
        start = pl.multiple_of(block * row_step, row_step)
        kv = kv_ref[pl.ds(start, key_rows), :]
    else:
        kv = kv_ref[...]
    keys = kv[:, :HD]
    vals = kv[:, HD:]
    lo = lo_ref[0]
    hi = hi_ref[0]
    t = t_ref[...]
    bias = jnp.where((lo <= t) & (t < hi), 0.0, -jnp.inf)
    for h in range(heads):
        q = q_ref[:, h * HD : (h + 1) * HD]
        s = lax.dot_general(
            q, keys, (((1,), (1,)), ((), ())), preferred_element_type=jnp.float32
        ) * HD ** (-0.5) + bias
        m = jnp.max(s, axis=1, keepdims=True)
        if sink:
            m = jnp.maximum(m, 0.0)
        p = jnp.exp(s - m)
        l = jnp.sum(p, axis=1, keepdims=True)
        if sink:
            l = l + jnp.exp(-m)
        o = jnp.dot(p.astype(jnp.bfloat16), vals, preferred_element_type=jnp.float32) / l
        r = g_ref[:, h : h + 1] * o
        if acc_ref is not None:
            r = acc_ref[:, h * HD : (h + 1) * HD] + r
        o_ref[:, h * HD : (h + 1) * HD] = r.astype(o_ref.dtype)


def branch(q, kv, lo, hi, t, gate, acc, *, sink, key_rows, row_step, out_dtype):
    rows, width = q.shape
    heads = width // HD
    blocks = rows // QB
    lo_map = (lambda i: (i, 0, 0)) if lo.shape[0] > 1 else (lambda i: (0, 0, 0))
    hi_map = (lambda i: (i, 0, 0)) if hi.shape[0] > 1 else (lambda i: (0, 0, 0))
    in_specs = [
        pl.BlockSpec((QB, width), lambda i: (i, 0)),
        pl.BlockSpec(kv.shape, lambda i: (0, 0)),
        pl.BlockSpec((1,) + lo.shape[1:], lo_map),
        pl.BlockSpec((1,) + hi.shape[1:], hi_map),
        pl.BlockSpec((QB, 1), lambda i: (i, 0)),
        pl.BlockSpec((QB, gate.shape[1]), lambda i: (i, 0)),
    ]
    args = [q, kv, lo, hi, t, gate]
    aliases = {}
    if acc is not None:
        in_specs.append(pl.BlockSpec((QB, width), lambda i: (i, 0)))
        args.append(acc)
        if acc.dtype == out_dtype:
            aliases = {len(args) - 1: 0}
    kernel = functools.partial(
        branch_kernel, sink=sink, key_rows=key_rows, row_step=row_step, heads=heads
    )
    flops = 4 * rows * heads * key_rows * HD
    cost = pl.CostEstimate(
        flops=flops,
        transcendentals=rows * heads * key_rows,
        bytes_accessed=q.size * 2 + kv.size * 2 + rows * width * 8,
    )
    return pl.pallas_call(
        kernel,
        grid=(blocks,),
        in_specs=in_specs,
        out_specs=pl.BlockSpec((QB, width), lambda i: (i, 0)),
        out_shape=jax.ShapeDtypeStruct((rows, width), out_dtype),
        input_output_aliases=aliases,
        compiler_params=pltpu.CompilerParams(
            dimension_semantics=("arbitrary",), vmem_limit_bytes=48 * 1024 * 1024
        ),
        cost_estimate=cost,
    )(*args)


def local(queries, keys, values, comp_k_weight, comp_v_weight, gate_logits, sel_tiles):
    ctx_count = lax.axis_size("ctx")
    head_count = lax.axis_size("head")
    ctx_index = lax.axis_index("ctx")
    head_index = lax.axis_index("head")
    local_rows = queries.shape[0]
    local_heads = queries.shape[1] // HD
    group_index = head_index * local_heads // (H // G)
    dev_rows = keys.shape[0]
    kv_rows = jnp.concatenate(
        [keys.reshape(dev_rows, G, HD), values.reshape(dev_rows, G, HD)], axis=2
    ).transpose(1, 0, 2)
    outbox_kv = jnp.repeat(kv_rows, (H // G) // local_heads, axis=0)
    group_kv = lax.all_to_all(outbox_kv, "head", 0, 0, tiled=True).reshape(
        local_rows, 2 * HD
    )
    tail_rows = shifted(group_kv[: KERN - STRIDE], "ctx", -1)
    extended = jnp.concatenate([group_kv, tail_rows], axis=0)
    comp_weight = jnp.concatenate(
        [
            lax.dynamic_slice_in_dim(comp_k_weight, group_index * HD, HD, 1),
            lax.dynamic_slice_in_dim(comp_v_weight, group_index * HD, HD, 1),
        ],
        axis=1,
    )
    comp_local = local_rows // STRIDE
    first_half = extended[:local_rows].reshape(comp_local, STRIDE, 2 * HD).astype(jnp.float32)
    second_half = (
        extended[STRIDE : STRIDE + local_rows]
        .reshape(comp_local, STRIDE, 2 * HD)
        .astype(jnp.float32)
    )
    compressed = (
        jnp.sum(first_half * comp_weight[None, :STRIDE], 1)
        + jnp.sum(second_half * comp_weight[None, STRIDE:], 1)
    ).astype(jnp.bfloat16)
    previous = shifted(group_kv[local_rows - WIN :], "ctx", 1)
    window_kv = jnp.concatenate([previous, group_kv], axis=0)

    block_count = local_rows // QB
    tiles_shard = local_rows // TILE
    share = (H // G) // local_heads
    part = head_index % share
    groups = [[g * share + i for i in range(share)] for g in range(head_count // share)]
    sel_share = CAP * TILE // share
    comp_share = comp_local // share
    group_tiles = lax.dynamic_slice_in_dim(sel_tiles, group_index * TOPK, TOPK, 1)
    own_tiles = lax.dynamic_slice_in_dim(group_tiles, ctx_index * block_count, block_count, 0)
    own_flat = own_tiles.reshape(-1)
    requests = group_tiles.reshape(ctx_count, block_count * TOPK)
    local_ids = ctx_index * tiles_shard + jnp.arange(tiles_shard)
    present = jnp.any(requests[:, :, None] == local_ids[None, None, :], axis=1)
    order_rank = jnp.cumsum(present.astype(jnp.int32), axis=1) - 1
    my_slot = part * sel_share // TILE
    my_row = part * sel_share % TILE
    picked = present & (order_rank == my_slot)
    tile_rows = lax.dynamic_slice_in_dim(
        group_kv.reshape(tiles_shard, TILE, 2 * HD), my_row, sel_share, 1
    )
    sel_part = jnp.einsum(
        "dt,tx->dx",
        picked.astype(jnp.bfloat16),
        tile_rows.reshape(tiles_shard, sel_share * 2 * HD),
        preferred_element_type=jnp.float32,
    ).astype(jnp.bfloat16).reshape(ctx_count, sel_share, 2 * HD)
    comp_part = jnp.broadcast_to(
        lax.dynamic_slice_in_dim(compressed, part * comp_share, comp_share, 0)[None],
        (ctx_count, comp_share, 2 * HD),
    )
    mail = jnp.concatenate([sel_part, comp_part], axis=1)
    arrived = lax.all_to_all(mail, "ctx", split_axis=0, concat_axis=0, tiled=True)
    gathered = lax.all_gather(arrived, "head", axis=0, axis_index_groups=groups)
    sel_kv = gathered[:, :, :sel_share].reshape(share * ctx_count * sel_share, 2 * HD)
    comp_kv = gathered[:, :, sel_share:].reshape(share * ctx_count * comp_share, 2 * HD)
    sel_rows = sel_kv.shape[0]
    comp_count = comp_kv.shape[0]
    all_ids = jnp.arange(ctx_count * tiles_shard).reshape(ctx_count, tiles_shard)
    wanted = jnp.any(own_flat[:, None, None] == all_ids[None, :, :], axis=0)
    wanted_rank = jnp.cumsum(wanted.astype(jnp.int32), axis=1) - 1
    chosen = wanted[:, None, :] & (wanted_rank[:, None, :] == jnp.arange(CAP)[None, :, None])
    slot_tile = jnp.sum(jnp.where(chosen, all_ids[:, None, :], 0), axis=2)
    slot_ok = jnp.any(chosen, axis=2)
    parts_per_slot = share // CAP
    row_in_tile = (
        jnp.arange(share)[:, None, None] % parts_per_slot * sel_share
        + jnp.arange(sel_share)[None, None, :]
    )
    key_tile = jnp.repeat(slot_tile, parts_per_slot, axis=1).T[:, :, None]
    key_pos = (key_tile * TILE + row_in_tile).reshape(-1)
    is_named = slot_ok[None] & jnp.any(
        own_tiles[:, :, None, None] == slot_tile[None, None], axis=1
    )
    key_named = jnp.broadcast_to(
        jnp.repeat(is_named, parts_per_slot, axis=2).transpose(0, 2, 1)[:, :, :, None],
        (block_count, share, ctx_count, sel_share),
    ).reshape(block_count, -1)
    sel_lo = jnp.where(key_named, key_pos[None, :], BIG).reshape(block_count, 1, sel_rows)
    never = jnp.full((1, 1, sel_rows), BIG, jnp.int32)

    comp_index = (
        jnp.arange(ctx_count)[None, :, None] * comp_local
        + jnp.arange(share)[:, None, None] * comp_share
        + jnp.arange(comp_share)[None, None, :]
    ).reshape(-1)
    comp_lo = (comp_index * STRIDE + KERN - 1).astype(jnp.int32).reshape(1, 1, comp_count)
    comp_hi = jnp.full((1, 1, comp_count), BIG, jnp.int32)

    win_rows = QB + WIN
    win_pos = (
        ctx_index * local_rows
        - WIN
        + jnp.arange(block_count)[:, None] * QB
        + jnp.arange(win_rows)[None, :]
    )
    win_lo = jnp.where(win_pos >= 0, win_pos, BIG).reshape(block_count, 1, win_rows)
    win_hi = (win_pos + WIN).reshape(block_count, 1, win_rows)

    positions = (ctx_index * local_rows + jnp.arange(local_rows, dtype=jnp.int32)).reshape(
        local_rows, 1
    )
    gate_values = jax.nn.sigmoid(gate_logits).transpose(0, 2, 1)

    acc = branch(
        queries, window_kv, win_lo, win_hi, positions, gate_values[2], None,
        sink=False, key_rows=win_rows, row_step=QB, out_dtype=jnp.float32,
    )
    acc = branch(
        queries, comp_kv, comp_lo, comp_hi, positions, gate_values[0], acc,
        sink=True, key_rows=comp_count, row_step=0, out_dtype=jnp.float32,
    )
    return branch(
        queries, sel_kv, sel_lo, never, positions, gate_values[1], acc,
        sink=True, key_rows=sel_rows, row_step=0, out_dtype=jnp.bfloat16,
    )


def solution(mesh):
    placed = (
        P("ctx", "head"),
        P(("ctx", "head"), None),
        P(("ctx", "head"), None),
        P(),
        P(),
        P(None, "head", "ctx"),
        P(),
    )
    return jax.shard_map(
        local, mesh=mesh, in_specs=placed, out_specs=P("ctx", "head"), check_vma=False
    )
```

```python
import functools

import jax
import jax.numpy as jnp
from jax import lax
from jax.experimental import pallas as pl
from jax.experimental.pallas import tpu as pltpu
from jax.sharding import PartitionSpec as P


H = 64
G = 4
HD = 128
KERN = 32
STRIDE = 16
TILE = 64
TOPK = 16
WIN = 512
QB = 256
CAP = 2
BIG = 1 << 30


def shifted(block, axis, distance):
    devices = range(lax.axis_size(axis))
    route = [(i - distance, i) for i in devices if i - distance in devices]
    return lax.ppermute(block, axis, route)


def branch_kernel(q_ref, kv_ref, lo_ref, hi_ref, t_ref, g_ref, *rest, sink, key_rows, row_step, heads):
    if len(rest) == 2:
        acc_ref, o_ref = rest
    else:
        acc_ref = None
        (o_ref,) = rest
    block = pl.program_id(0)
    if row_step:
        start = pl.multiple_of(block * row_step, row_step)
        kv = kv_ref[pl.ds(start, key_rows), :]
    else:
        kv = kv_ref[...]
    keys = kv[:, :HD]
    vals = kv[:, HD:]
    lo = lo_ref[0]
    hi = hi_ref[0]
    t = t_ref[...]
    bias = jnp.where((lo <= t) & (t < hi), 0.0, -jnp.inf)
    for h in range(heads):
        q = q_ref[:, h * HD : (h + 1) * HD]
        s = lax.dot_general(
            q, keys, (((1,), (1,)), ((), ())), preferred_element_type=jnp.float32
        ) * HD ** (-0.5) + bias
        m = jnp.max(s, axis=1, keepdims=True)
        if sink:
            m = jnp.maximum(m, 0.0)
        p = jnp.exp(s - m)
        l = jnp.sum(p, axis=1, keepdims=True)
        if sink:
            l = l + jnp.exp(-m)
        o = jnp.dot(p.astype(jnp.bfloat16), vals, preferred_element_type=jnp.float32) / l
        r = g_ref[:, h : h + 1] * o
        if acc_ref is not None:
            r = acc_ref[:, h * HD : (h + 1) * HD] + r
        o_ref[:, h * HD : (h + 1) * HD] = r.astype(o_ref.dtype)


def branch(q, kv, lo, hi, t, gate, acc, *, sink, key_rows, row_step, out_dtype):
    rows, width = q.shape
    heads = width // HD
    blocks = rows // QB
    lo_map = (lambda i: (i, 0, 0)) if lo.shape[0] > 1 else (lambda i: (0, 0, 0))
    hi_map = (lambda i: (i, 0, 0)) if hi.shape[0] > 1 else (lambda i: (0, 0, 0))
    in_specs = [
        pl.BlockSpec((QB, width), lambda i: (i, 0)),
        pl.BlockSpec(kv.shape, lambda i: (0, 0)),
        pl.BlockSpec((1,) + lo.shape[1:], lo_map),
        pl.BlockSpec((1,) + hi.shape[1:], hi_map),
        pl.BlockSpec((QB, 1), lambda i: (i, 0)),
        pl.BlockSpec((QB, gate.shape[1]), lambda i: (i, 0)),
    ]
    args = [q, kv, lo, hi, t, gate]
    aliases = {}
    if acc is not None:
        in_specs.append(pl.BlockSpec((QB, width), lambda i: (i, 0)))
        args.append(acc)
        if acc.dtype == out_dtype:
            aliases = {len(args) - 1: 0}
    kernel = functools.partial(
        branch_kernel, sink=sink, key_rows=key_rows, row_step=row_step, heads=heads
    )
    flops = 4 * rows * heads * key_rows * HD
    cost = pl.CostEstimate(
        flops=flops,
        transcendentals=rows * heads * key_rows,
        bytes_accessed=q.size * 2 + kv.size * 2 + rows * width * 8,
    )
    return pl.pallas_call(
        kernel,
        grid=(blocks,),
        in_specs=in_specs,
        out_specs=pl.BlockSpec((QB, width), lambda i: (i, 0)),
        out_shape=jax.ShapeDtypeStruct((rows, width), out_dtype),
        input_output_aliases=aliases,
        compiler_params=pltpu.CompilerParams(
            dimension_semantics=("arbitrary",), vmem_limit_bytes=48 * 1024 * 1024
        ),
        cost_estimate=cost,
    )(*args)


def local(queries, keys, values, comp_k_weight, comp_v_weight, gate_logits, sel_tiles):
    ctx_count = lax.axis_size("ctx")
    head_count = lax.axis_size("head")
    ctx_index = lax.axis_index("ctx")
    head_index = lax.axis_index("head")
    local_rows = queries.shape[0]
    local_heads = queries.shape[1] // HD
    group_index = head_index * local_heads // (H // G)
    dev_rows = keys.shape[0]
    kv_rows = jnp.concatenate(
        [keys.reshape(dev_rows, G, HD), values.reshape(dev_rows, G, HD)], axis=2
    ).transpose(1, 0, 2)
    outbox_kv = jnp.repeat(kv_rows, (H // G) // local_heads, axis=0)
    group_kv = lax.all_to_all(outbox_kv, "head", 0, 0, tiled=True).reshape(
        local_rows, 2 * HD
    )
    previous = shifted(group_kv[local_rows - WIN :], "ctx", 1)
    window_kv = jnp.concatenate([previous, group_kv], axis=0)
    extended = window_kv[WIN - STRIDE :]
    comp_weight = jnp.concatenate(
        [
            lax.dynamic_slice_in_dim(comp_k_weight, group_index * HD, HD, 1),
            lax.dynamic_slice_in_dim(comp_v_weight, group_index * HD, HD, 1),
        ],
        axis=1,
    )
    comp_local = local_rows // STRIDE
    first_half = extended[:local_rows].reshape(comp_local, STRIDE, 2 * HD).astype(jnp.float32)
    second_half = (
        extended[STRIDE : STRIDE + local_rows]
        .reshape(comp_local, STRIDE, 2 * HD)
        .astype(jnp.float32)
    )
    compressed = (
        jnp.sum(first_half * comp_weight[None, :STRIDE], 1)
        + jnp.sum(second_half * comp_weight[None, STRIDE:], 1)
    ).astype(jnp.bfloat16)

    block_count = local_rows // QB
    tiles_shard = local_rows // TILE
    share = (H // G) // local_heads
    part = head_index % share
    groups = [[g * share + i for i in range(share)] for g in range(head_count // share)]
    sel_share = CAP * TILE // share
    comp_share = comp_local // share
    group_tiles = lax.dynamic_slice_in_dim(sel_tiles, group_index * TOPK, TOPK, 1)
    own_tiles = lax.dynamic_slice_in_dim(group_tiles, ctx_index * block_count, block_count, 0)
    own_flat = own_tiles.reshape(-1)
    requests = group_tiles.reshape(ctx_count, block_count * TOPK)
    local_ids = ctx_index * tiles_shard + jnp.arange(tiles_shard)
    present = jnp.any(requests[:, :, None] == local_ids[None, None, :], axis=1)
    order_rank = jnp.cumsum(present.astype(jnp.int32), axis=1) - 1
    my_slot = part * sel_share // TILE
    my_row = part * sel_share % TILE
    picked = present & (order_rank == my_slot)
    tile_rows = lax.dynamic_slice_in_dim(
        group_kv.reshape(tiles_shard, TILE, 2 * HD), my_row, sel_share, 1
    )
    sel_part = jnp.einsum(
        "dt,tx->dx",
        picked.astype(jnp.bfloat16),
        tile_rows.reshape(tiles_shard, sel_share * 2 * HD),
        preferred_element_type=jnp.float32,
    ).astype(jnp.bfloat16).reshape(ctx_count, sel_share, 2 * HD)
    comp_part = jnp.broadcast_to(
        lax.dynamic_slice_in_dim(compressed, part * comp_share, comp_share, 0)[None],
        (ctx_count, comp_share, 2 * HD),
    )
    mail = jnp.concatenate([sel_part, comp_part], axis=1)
    arrived = lax.all_to_all(mail, "ctx", split_axis=0, concat_axis=0, tiled=True)
    gathered = lax.all_gather(arrived, "head", axis=0, axis_index_groups=groups)
    sel_kv = gathered[:, :, :sel_share].reshape(share * ctx_count * sel_share, 2 * HD)
    comp_kv = gathered[:, :, sel_share:].reshape(share * ctx_count * comp_share, 2 * HD)
    sel_rows = sel_kv.shape[0]
    comp_count = comp_kv.shape[0]
    all_ids = jnp.arange(ctx_count * tiles_shard).reshape(ctx_count, tiles_shard)
    wanted = jnp.any(own_flat[:, None, None] == all_ids[None, :, :], axis=0)
    wanted_rank = jnp.cumsum(wanted.astype(jnp.int32), axis=1) - 1
    chosen = wanted[:, None, :] & (wanted_rank[:, None, :] == jnp.arange(CAP)[None, :, None])
    slot_tile = jnp.sum(jnp.where(chosen, all_ids[:, None, :], 0), axis=2)
    slot_ok = jnp.any(chosen, axis=2)
    parts_per_slot = share // CAP
    row_in_tile = (
        jnp.arange(share)[:, None, None] % parts_per_slot * sel_share
        + jnp.arange(sel_share)[None, None, :]
    )
    key_tile = jnp.repeat(slot_tile, parts_per_slot, axis=1).T[:, :, None]
    key_pos = (key_tile * TILE + row_in_tile).reshape(-1)
    is_named = slot_ok[None] & jnp.any(
        own_tiles[:, :, None, None] == slot_tile[None, None], axis=1
    )
    key_named = jnp.broadcast_to(
        jnp.repeat(is_named, parts_per_slot, axis=2).transpose(0, 2, 1)[:, :, :, None],
        (block_count, share, ctx_count, sel_share),
    ).reshape(block_count, -1)
    sel_lo = jnp.where(key_named, key_pos[None, :], BIG).reshape(block_count, 1, sel_rows)
    never = jnp.full((1, 1, sel_rows), BIG, jnp.int32)

    comp_index = (
        jnp.arange(ctx_count)[None, :, None] * comp_local
        + jnp.arange(share)[:, None, None] * comp_share
        + jnp.arange(comp_share)[None, None, :]
    ).reshape(-1)
    comp_block = comp_index - 1
    comp_lo = jnp.where(comp_block >= 0, comp_block * STRIDE + KERN - 1, BIG)
    comp_lo = comp_lo.astype(jnp.int32).reshape(1, 1, comp_count)
    comp_hi = jnp.full((1, 1, comp_count), BIG, jnp.int32)

    win_rows = QB + WIN
    win_pos = (
        ctx_index * local_rows
        - WIN
        + jnp.arange(block_count)[:, None] * QB
        + jnp.arange(win_rows)[None, :]
    )
    win_lo = jnp.where(win_pos >= 0, win_pos, BIG).reshape(block_count, 1, win_rows)
    win_hi = (win_pos + WIN).reshape(block_count, 1, win_rows)

    positions = (ctx_index * local_rows + jnp.arange(local_rows, dtype=jnp.int32)).reshape(
        local_rows, 1
    )
    gate_values = jax.nn.sigmoid(gate_logits).transpose(0, 2, 1)

    acc = branch(
        queries, window_kv, win_lo, win_hi, positions, gate_values[2], None,
        sink=False, key_rows=win_rows, row_step=QB, out_dtype=jnp.float32,
    )
    acc = branch(
        queries, comp_kv, comp_lo, comp_hi, positions, gate_values[0], acc,
        sink=True, key_rows=comp_count, row_step=0, out_dtype=jnp.float32,
    )
    return branch(
        queries, sel_kv, sel_lo, never, positions, gate_values[1], acc,
        sink=True, key_rows=sel_rows, row_step=0, out_dtype=jnp.bfloat16,
    )


def solution(mesh):
    placed = (
        P("ctx", "head"),
        P(("ctx", "head"), None),
        P(("ctx", "head"), None),
        P(),
        P(),
        P(None, "head", "ctx"),
        P(),
    )

    return jax.shard_map(
        local, mesh=mesh, in_specs=placed, out_specs=P("ctx", "head"), check_vma=False
    )
```

```python
import functools

import jax
import jax.numpy as jnp
from jax import lax
from jax.experimental import pallas as pl
from jax.experimental.pallas import tpu as pltpu
from jax.sharding import PartitionSpec as P


H = 64
G = 4
HD = 128
KERN = 32
STRIDE = 16
TILE = 64
TOPK = 16
WIN = 512
QB = 256
CAP = 2
BIG = 1 << 30
CORES = 2


def shifted(block, axis, distance):
    devices = range(lax.axis_size(axis))
    route = [(i - distance, i) for i in devices if i - distance in devices]
    return lax.ppermute(block, axis, route)


def branch_kernel(q_ref, kv_ref, lo_ref, hi_ref, t_ref, g_ref, *rest, sink, key_rows, row_step, heads):
    if len(rest) == 2:
        acc_ref, o_ref = rest
    else:
        acc_ref = None
        (o_ref,) = rest
    block = pl.program_id(0)
    if row_step:
        start = pl.multiple_of(block * row_step, row_step)
        kv = kv_ref[pl.ds(start, key_rows), :]
    else:
        kv = kv_ref[...]
    keys = kv[:, :HD]
    vals = kv[:, HD:]
    lo = lo_ref[0]
    hi = hi_ref[0]
    t = t_ref[...]
    bias = jnp.where((lo <= t) & (t < hi), 0.0, -jnp.inf)
    for h in range(heads):
        q = q_ref[:, h * HD : (h + 1) * HD]
        s = lax.dot_general(
            q, keys, (((1,), (1,)), ((), ())), preferred_element_type=jnp.float32
        ) * HD ** (-0.5) + bias
        m = jnp.max(s, axis=1, keepdims=True)
        if sink:
            m = jnp.maximum(m, 0.0)
        p = jnp.exp(s - m)
        l = jnp.sum(p, axis=1, keepdims=True)
        if sink:
            l = l + jnp.exp(-m)
        o = jnp.dot(p.astype(jnp.bfloat16), vals, preferred_element_type=jnp.float32) / l
        r = g_ref[:, h : h + 1] * o
        if acc_ref is not None:
            r = acc_ref[:, h * HD : (h + 1) * HD] + r
        o_ref[:, h * HD : (h + 1) * HD] = r.astype(o_ref.dtype)


def branch(q, kv, lo, hi, t, gate, acc, *, sink, key_rows, row_step, out_dtype):
    rows, width = q.shape
    heads = width // HD
    blocks = rows // QB
    lo_map = (lambda i: (i, 0, 0)) if lo.shape[0] > 1 else (lambda i: (0, 0, 0))
    hi_map = (lambda i: (i, 0, 0)) if hi.shape[0] > 1 else (lambda i: (0, 0, 0))
    in_specs = [
        pl.BlockSpec((QB, width), lambda i: (i, 0)),
        pl.BlockSpec(kv.shape, lambda i: (0, 0)),
        pl.BlockSpec((1,) + lo.shape[1:], lo_map),
        pl.BlockSpec((1,) + hi.shape[1:], hi_map),
        pl.BlockSpec((QB, 1), lambda i: (i, 0)),
        pl.BlockSpec((QB, gate.shape[1]), lambda i: (i, 0)),
    ]
    args = [q, kv, lo, hi, t, gate]
    aliases = {}
    if acc is not None:
        in_specs.append(pl.BlockSpec((QB, width), lambda i: (i, 0)))
        args.append(acc)
        if acc.dtype == out_dtype:
            aliases = {len(args) - 1: 0}
    kernel = functools.partial(
        branch_kernel, sink=sink, key_rows=key_rows, row_step=row_step, heads=heads
    )
    flops = 4 * rows * heads * key_rows * HD
    cost = pl.CostEstimate(
        flops=flops,
        transcendentals=rows * heads * key_rows,
        bytes_accessed=q.size * 2 + kv.size * 2 + rows * width * 8,
    )
    return pl.pallas_call(
        kernel,
        grid=(blocks,),
        in_specs=in_specs,
        out_specs=pl.BlockSpec((QB, width), lambda i: (i, 0)),
        out_shape=jax.ShapeDtypeStruct((rows, width), out_dtype),
        input_output_aliases=aliases,
        compiler_params=pltpu.CompilerParams(
            dimension_semantics=("arbitrary",), vmem_limit_bytes=48 * 1024 * 1024
        ),
        cost_estimate=cost,
    )(*args)


def local(queries, keys, values, comp_k_weight, comp_v_weight, gate_logits, sel_tiles):
    ctx_count = lax.axis_size("ctx")
    head_count = lax.axis_size("head")
    ctx_index = lax.axis_index("ctx")
    head_index = lax.axis_index("head")
    local_rows = queries.shape[0]
    local_heads = queries.shape[1] // HD
    group_index = head_index * local_heads // (H // G)
    dev_rows = keys.shape[0]
    kv_rows = jnp.concatenate(
        [keys.reshape(dev_rows, G, HD), values.reshape(dev_rows, G, HD)], axis=2
    ).transpose(1, 0, 2)
    outbox_kv = jnp.repeat(kv_rows, (H // G) // local_heads, axis=0)
    group_kv = lax.all_to_all(outbox_kv, "head", 0, 0, tiled=True).reshape(
        local_rows, 2 * HD
    )
    previous = shifted(group_kv[local_rows - WIN :], "ctx", 1)
    window_kv = jnp.concatenate([previous, group_kv], axis=0)
    extended = window_kv[WIN - STRIDE :]
    comp_weight = jnp.concatenate(
        [
            lax.dynamic_slice_in_dim(comp_k_weight, group_index * HD, HD, 1),
            lax.dynamic_slice_in_dim(comp_v_weight, group_index * HD, HD, 1),
        ],
        axis=1,
    )
    comp_local = local_rows // STRIDE
    first_half = extended[:local_rows].reshape(comp_local, STRIDE, 2 * HD).astype(jnp.float32)
    second_half = (
        extended[STRIDE : STRIDE + local_rows]
        .reshape(comp_local, STRIDE, 2 * HD)
        .astype(jnp.float32)
    )
    compressed = (
        jnp.sum(first_half * comp_weight[None, :STRIDE], 1)
        + jnp.sum(second_half * comp_weight[None, STRIDE:], 1)
    ).astype(jnp.bfloat16)

    block_count = local_rows // QB
    tiles_shard = local_rows // TILE
    share = CORES
    part = head_index % share
    groups = [[g * share + i for i in range(share)] for g in range(head_count // share)]
    sel_share = CAP * TILE // share
    comp_share = comp_local // share
    group_tiles = lax.dynamic_slice_in_dim(sel_tiles, group_index * TOPK, TOPK, 1)
    own_tiles = lax.dynamic_slice_in_dim(group_tiles, ctx_index * block_count, block_count, 0)
    own_flat = own_tiles.reshape(-1)
    requests = group_tiles.reshape(ctx_count, block_count * TOPK)
    local_ids = ctx_index * tiles_shard + jnp.arange(tiles_shard)
    present = jnp.any(requests[:, :, None] == local_ids[None, None, :], axis=1)
    order_rank = jnp.cumsum(present.astype(jnp.int32), axis=1) - 1
    my_slot = part * sel_share // TILE
    my_row = part * sel_share % TILE
    picked = present & (order_rank == my_slot)
    tile_rows = lax.dynamic_slice_in_dim(
        group_kv.reshape(tiles_shard, TILE, 2 * HD), my_row, sel_share, 1
    )
    sel_part = jnp.einsum(
        "dt,tx->dx",
        picked.astype(jnp.bfloat16),
        tile_rows.reshape(tiles_shard, sel_share * 2 * HD),
        preferred_element_type=jnp.float32,
    ).astype(jnp.bfloat16).reshape(ctx_count, sel_share, 2 * HD)
    comp_part = jnp.broadcast_to(
        lax.dynamic_slice_in_dim(compressed, part * comp_share, comp_share, 0)[None],
        (ctx_count, comp_share, 2 * HD),
    )
    mail = jnp.concatenate([sel_part, comp_part], axis=1)
    arrived = lax.all_to_all(mail, "ctx", split_axis=0, concat_axis=0, tiled=True)
    spread = jnp.broadcast_to(arrived[None], (share,) + arrived.shape).reshape(
        (share * ctx_count,) + arrived.shape[1:]
    )
    gathered = lax.all_to_all(
        spread, "head", 0, 0, axis_index_groups=groups, tiled=True
    ).reshape((share,) + arrived.shape)
    sel_kv = gathered[:, :, :sel_share].reshape(share * ctx_count * sel_share, 2 * HD)
    comp_kv = gathered[:, :, sel_share:].reshape(share * ctx_count * comp_share, 2 * HD)
    sel_rows = sel_kv.shape[0]
    comp_count = comp_kv.shape[0]
    all_ids = jnp.arange(ctx_count * tiles_shard).reshape(ctx_count, tiles_shard)
    wanted = jnp.any(own_flat[:, None, None] == all_ids[None, :, :], axis=0)
    wanted_rank = jnp.cumsum(wanted.astype(jnp.int32), axis=1) - 1
    chosen = wanted[:, None, :] & (wanted_rank[:, None, :] == jnp.arange(CAP)[None, :, None])
    slot_tile = jnp.sum(jnp.where(chosen, all_ids[:, None, :], 0), axis=2)
    slot_ok = jnp.any(chosen, axis=2)
    parts_per_slot = share // CAP
    row_in_tile = (
        jnp.arange(share)[:, None, None] % parts_per_slot * sel_share
        + jnp.arange(sel_share)[None, None, :]
    )
    key_tile = jnp.repeat(slot_tile, parts_per_slot, axis=1).T[:, :, None]
    key_pos = (key_tile * TILE + row_in_tile).reshape(-1)
    is_named = slot_ok[None] & jnp.any(
        own_tiles[:, :, None, None] == slot_tile[None, None], axis=1
    )
    key_named = jnp.broadcast_to(
        jnp.repeat(is_named, parts_per_slot, axis=2).transpose(0, 2, 1)[:, :, :, None],
        (block_count, share, ctx_count, sel_share),
    ).reshape(block_count, -1)
    sel_lo = jnp.where(key_named, key_pos[None, :], BIG).reshape(block_count, 1, sel_rows)
    never = jnp.full((1, 1, sel_rows), BIG, jnp.int32)

    comp_index = (
        jnp.arange(ctx_count)[None, :, None] * comp_local
        + jnp.arange(share)[:, None, None] * comp_share
        + jnp.arange(comp_share)[None, None, :]
    ).reshape(-1)
    comp_block = comp_index - 1
    comp_lo = jnp.where(comp_block >= 0, comp_block * STRIDE + KERN - 1, BIG)
    comp_lo = comp_lo.astype(jnp.int32).reshape(1, 1, comp_count)
    comp_hi = jnp.full((1, 1, comp_count), BIG, jnp.int32)

    win_rows = QB + WIN
    win_pos = (
        ctx_index * local_rows
        - WIN
        + jnp.arange(block_count)[:, None] * QB
        + jnp.arange(win_rows)[None, :]
    )
    win_lo = jnp.where(win_pos >= 0, win_pos, BIG).reshape(block_count, 1, win_rows)
    win_hi = (win_pos + WIN).reshape(block_count, 1, win_rows)

    positions = (ctx_index * local_rows + jnp.arange(local_rows, dtype=jnp.int32)).reshape(
        local_rows, 1
    )
    gate_values = jax.nn.sigmoid(gate_logits).transpose(0, 2, 1)

    acc = branch(
        queries, window_kv, win_lo, win_hi, positions, gate_values[2], None,
        sink=False, key_rows=win_rows, row_step=QB, out_dtype=jnp.float32,
    )
    acc = branch(
        queries, comp_kv, comp_lo, comp_hi, positions, gate_values[0], acc,
        sink=True, key_rows=comp_count, row_step=0, out_dtype=jnp.float32,
    )
    return branch(
        queries, sel_kv, sel_lo, never, positions, gate_values[1], acc,
        sink=True, key_rows=sel_rows, row_step=0, out_dtype=jnp.bfloat16,
    )


def solution(mesh):
    placed = (
        P("ctx", "head"),
        P(("ctx", "head"), None),
        P(("ctx", "head"), None),
        P(),
        P(),
        P(None, "head", "ctx"),
        P(),
    )

    return jax.shard_map(
        local, mesh=mesh, in_specs=placed, out_specs=P("ctx", "head"), check_vma=False
    )
```

```python
import functools

import jax
import jax.numpy as jnp
from jax import lax
from jax.experimental import pallas as pl
from jax.experimental.pallas import tpu as pltpu
from jax.sharding import PartitionSpec as P


H = 64
G = 4
HD = 128
KERN = 32
STRIDE = 16
TILE = 64
TOPK = 16
WIN = 512
QB = 256
CAP = 2
BIG = 1 << 30
CORES = 2


def shifted(block, axis, distance):
    devices = range(lax.axis_size(axis))
    route = [(i - distance, i) for i in devices if i - distance in devices]
    return lax.ppermute(block, axis, route)


def branch_kernel(*refs, sink, key_rows, row_step, heads, picks, with_acc):
    if picks:
        pick_ref, refs = refs[0], refs[1:]
        refs, pool_ref = refs[:-1], refs[-1]
    q_ref, kv_ref, lo_ref, hi_ref, t_ref, g_ref = refs[:6]
    if with_acc:
        acc_ref, o_ref = refs[6:]
    else:
        acc_ref = None
        (o_ref,) = refs[6:]
    block = pl.program_id(0)
    if picks:
        for k in range(picks):
            begin = pl.multiple_of(pick_ref[block, k] * TILE, TILE)
            pool_ref[k * TILE : (k + 1) * TILE, :] = kv_ref[pl.ds(begin, TILE), :]
        kv = pool_ref[...]
    elif row_step:
        start = pl.multiple_of(block * row_step, row_step)
        kv = kv_ref[pl.ds(start, key_rows), :]
    else:
        kv = kv_ref[...]
    keys = kv[:, :HD]
    vals = kv[:, HD:]
    lo = lo_ref[0]
    hi = hi_ref[0]
    t = t_ref[...]
    bias = jnp.where((lo <= t) & (t < hi), 0.0, -jnp.inf)
    for h in range(heads):
        q = q_ref[:, h * HD : (h + 1) * HD]
        s = lax.dot_general(
            q, keys, (((1,), (1,)), ((), ())), preferred_element_type=jnp.float32
        ) * HD ** (-0.5) + bias
        m = jnp.max(s, axis=1, keepdims=True)
        if sink:
            m = jnp.maximum(m, 0.0)
        p = jnp.exp(s - m)
        l = jnp.sum(p, axis=1, keepdims=True)
        if sink:
            l = l + jnp.exp(-m)
        o = jnp.dot(p.astype(jnp.bfloat16), vals, preferred_element_type=jnp.float32) / l
        r = g_ref[:, h : h + 1] * o
        if acc_ref is not None:
            r = acc_ref[:, h * HD : (h + 1) * HD] + r
        o_ref[:, h * HD : (h + 1) * HD] = r.astype(o_ref.dtype)


def branch(q, kv, lo, hi, t, gate, acc, *, sink, key_rows, row_step, out_dtype, pick=None):
    rows, width = q.shape
    heads = width // HD
    blocks = rows // QB
    lo_map = (lambda i, *_: (i, 0, 0)) if lo.shape[0] > 1 else (lambda i, *_: (0, 0, 0))
    hi_map = (lambda i, *_: (i, 0, 0)) if hi.shape[0] > 1 else (lambda i, *_: (0, 0, 0))
    row_map = lambda i, *_: (i, 0)
    in_specs = [
        pl.BlockSpec((QB, width), row_map),
        pl.BlockSpec(kv.shape, lambda i, *_: (0, 0)),
        pl.BlockSpec((1,) + lo.shape[1:], lo_map),
        pl.BlockSpec((1,) + hi.shape[1:], hi_map),
        pl.BlockSpec((QB, 1), row_map),
        pl.BlockSpec((QB, gate.shape[1]), row_map),
    ]
    args = [q, kv, lo, hi, t, gate]
    aliases = {}
    prefix = 0 if pick is None else 1
    if acc is not None:
        in_specs.append(pl.BlockSpec((QB, width), row_map))
        args.append(acc)
        if acc.dtype == out_dtype:
            aliases = {len(args) - 1 + prefix: 0}
    picks = 0 if pick is None else pick.shape[1]
    scratch = [] if pick is None else [pltpu.VMEM((key_rows, kv.shape[1]), kv.dtype)]
    kernel = functools.partial(
        branch_kernel, sink=sink, key_rows=key_rows, row_step=row_step, heads=heads,
        picks=picks, with_acc=acc is not None,
    )
    flops = 4 * rows * heads * key_rows * HD
    cost = pl.CostEstimate(
        flops=flops,
        transcendentals=rows * heads * key_rows,
        bytes_accessed=q.size * 2 + kv.size * 2 + rows * width * 8,
    )
    if pick is not None:
        args = [pick] + args
    return pl.pallas_call(
        kernel,
        grid_spec=pltpu.PrefetchScalarGridSpec(
            num_scalar_prefetch=prefix,
            grid=(blocks,),
            in_specs=in_specs,
            out_specs=pl.BlockSpec((QB, width), row_map),
            scratch_shapes=scratch,
        ),
        out_shape=jax.ShapeDtypeStruct((rows, width), out_dtype),
        input_output_aliases=aliases,
        compiler_params=pltpu.CompilerParams(
            dimension_semantics=("arbitrary",), vmem_limit_bytes=48 * 1024 * 1024
        ),
        cost_estimate=cost,
    )(*args)


def local(queries, keys, values, comp_k_weight, comp_v_weight, gate_logits, sel_tiles):
    ctx_count = lax.axis_size("ctx")
    head_count = lax.axis_size("head")
    ctx_index = lax.axis_index("ctx")
    head_index = lax.axis_index("head")
    local_rows = queries.shape[0]
    local_heads = queries.shape[1] // HD
    group_index = head_index * local_heads // (H // G)
    dev_rows = keys.shape[0]
    kv_rows = jnp.concatenate(
        [keys.reshape(dev_rows, G, HD), values.reshape(dev_rows, G, HD)], axis=2
    ).transpose(1, 0, 2)
    outbox_kv = jnp.repeat(kv_rows, (H // G) // local_heads, axis=0)
    group_kv = lax.all_to_all(outbox_kv, "head", 0, 0, tiled=True).reshape(
        local_rows, 2 * HD
    )
    previous = shifted(group_kv[local_rows - WIN :], "ctx", 1)
    window_kv = jnp.concatenate([previous, group_kv], axis=0)
    extended = window_kv[WIN - STRIDE :]
    comp_weight = jnp.concatenate(
        [
            lax.dynamic_slice_in_dim(comp_k_weight, group_index * HD, HD, 1),
            lax.dynamic_slice_in_dim(comp_v_weight, group_index * HD, HD, 1),
        ],
        axis=1,
    )
    comp_local = local_rows // STRIDE
    first_half = extended[:local_rows].reshape(comp_local, STRIDE, 2 * HD).astype(jnp.float32)
    second_half = (
        extended[STRIDE : STRIDE + local_rows]
        .reshape(comp_local, STRIDE, 2 * HD)
        .astype(jnp.float32)
    )
    compressed = (
        jnp.sum(first_half * comp_weight[None, :STRIDE], 1)
        + jnp.sum(second_half * comp_weight[None, STRIDE:], 1)
    ).astype(jnp.bfloat16)

    block_count = local_rows // QB
    tiles_shard = local_rows // TILE
    share = CORES
    part = head_index % share
    groups = [[g * share + i for i in range(share)] for g in range(head_count // share)]
    sel_share = CAP * TILE // share
    comp_share = comp_local // share
    group_tiles = lax.dynamic_slice_in_dim(sel_tiles, group_index * TOPK, TOPK, 1)
    own_tiles = lax.dynamic_slice_in_dim(group_tiles, ctx_index * block_count, block_count, 0)
    own_flat = own_tiles.reshape(-1)
    requests = group_tiles.reshape(ctx_count, block_count * TOPK)
    local_ids = ctx_index * tiles_shard + jnp.arange(tiles_shard)
    present = jnp.any(requests[:, :, None] == local_ids[None, None, :], axis=1)
    order_rank = jnp.cumsum(present.astype(jnp.int32), axis=1) - 1
    my_slot = part * sel_share // TILE
    my_row = part * sel_share % TILE
    picked = present & (order_rank == my_slot)
    tile_rows = lax.dynamic_slice_in_dim(
        group_kv.reshape(tiles_shard, TILE, 2 * HD), my_row, sel_share, 1
    )
    sel_part = jnp.einsum(
        "dt,tx->dx",
        picked.astype(jnp.bfloat16),
        tile_rows.reshape(tiles_shard, sel_share * 2 * HD),
        preferred_element_type=jnp.float32,
    ).astype(jnp.bfloat16).reshape(ctx_count, sel_share, 2 * HD)
    comp_part = jnp.broadcast_to(
        lax.dynamic_slice_in_dim(compressed, part * comp_share, comp_share, 0)[None],
        (ctx_count, comp_share, 2 * HD),
    )
    mail = jnp.concatenate([sel_part, comp_part], axis=1)
    arrived = lax.all_to_all(mail, "ctx", split_axis=0, concat_axis=0, tiled=True)
    spread = jnp.broadcast_to(arrived[None], (share,) + arrived.shape).reshape(
        (share * ctx_count,) + arrived.shape[1:]
    )
    gathered = lax.all_to_all(
        spread, "head", 0, 0, axis_index_groups=groups, tiled=True
    ).reshape((share,) + arrived.shape)
    sel_kv = gathered[:, :, :sel_share].reshape(share * ctx_count * sel_share, 2 * HD)
    comp_kv = gathered[:, :, sel_share:].reshape(share * ctx_count * comp_share, 2 * HD)
    comp_count = comp_kv.shape[0]
    all_ids = jnp.arange(ctx_count * tiles_shard).reshape(ctx_count, tiles_shard)
    wanted = jnp.any(own_flat[:, None, None] == all_ids[None, :, :], axis=0)
    wanted_rank = jnp.cumsum(wanted.astype(jnp.int32), axis=1) - 1
    chosen = wanted[:, None, :] & (wanted_rank[:, None, :] == jnp.arange(CAP)[None, :, None])
    slot_tile = jnp.sum(jnp.where(chosen, all_ids[:, None, :], 0), axis=2)
    slot_ok = jnp.any(chosen, axis=2)
    parts_per_slot = share // CAP
    row_in_tile = (
        jnp.arange(share)[:, None, None] % parts_per_slot * sel_share
        + jnp.arange(sel_share)[None, None, :]
    )
    key_tile = jnp.repeat(slot_tile, parts_per_slot, axis=1).T[:, :, None]
    key_pos = (key_tile * TILE + row_in_tile).reshape(-1)
    is_named = slot_ok[None] & jnp.any(
        own_tiles[:, :, None, None] == slot_tile[None, None], axis=1
    )
    key_named = jnp.broadcast_to(
        jnp.repeat(is_named, parts_per_slot, axis=2).transpose(0, 2, 1)[:, :, :, None],
        (block_count, share, ctx_count, sel_share),
    ).reshape(block_count, -1)
    slot_named = key_named.reshape(block_count, share * ctx_count, TILE)[:, :, 0]
    slot_base = key_pos.reshape(share * ctx_count, TILE)[:, 0]
    slot_rank = jnp.cumsum(slot_named.astype(jnp.int32), axis=1) - 1
    hit = slot_named[:, None, :] & (slot_rank[:, None, :] == jnp.arange(TOPK)[None, :, None])
    pick = jnp.sum(
        jnp.where(hit, jnp.arange(share * ctx_count)[None, None, :], 0), axis=2
    ).astype(jnp.int32)
    pick_base = jnp.sum(jnp.where(hit, slot_base[None, None, :], 0), axis=2)
    pick_ok = jnp.any(hit, axis=2)
    pick_pos = pick_base[:, :, None] + jnp.arange(TILE)[None, None, :]
    sel_lo = jnp.where(pick_ok[:, :, None], pick_pos, BIG).reshape(block_count, 1, TOPK * TILE)
    never = jnp.full((1, 1, TOPK * TILE), BIG, jnp.int32)

    comp_index = (
        jnp.arange(ctx_count)[None, :, None] * comp_local
        + jnp.arange(share)[:, None, None] * comp_share
        + jnp.arange(comp_share)[None, None, :]
    ).reshape(-1)
    comp_block = comp_index - 1
    comp_lo = jnp.where(comp_block >= 0, comp_block * STRIDE + KERN - 1, BIG)
    comp_lo = comp_lo.astype(jnp.int32).reshape(1, 1, comp_count)
    comp_hi = jnp.full((1, 1, comp_count), BIG, jnp.int32)

    win_rows = QB + WIN
    win_pos = (
        ctx_index * local_rows
        - WIN
        + jnp.arange(block_count)[:, None] * QB
        + jnp.arange(win_rows)[None, :]
    )
    win_lo = jnp.where(win_pos >= 0, win_pos, BIG).reshape(block_count, 1, win_rows)
    win_hi = (win_pos + WIN).reshape(block_count, 1, win_rows)

    positions = (ctx_index * local_rows + jnp.arange(local_rows, dtype=jnp.int32)).reshape(
        local_rows, 1
    )
    gate_values = jax.nn.sigmoid(gate_logits).transpose(0, 2, 1)

    acc = branch(
        queries, window_kv, win_lo, win_hi, positions, gate_values[2], None,
        sink=False, key_rows=win_rows, row_step=QB, out_dtype=jnp.float32,
    )
    acc = branch(
        queries, comp_kv, comp_lo, comp_hi, positions, gate_values[0], acc,
        sink=True, key_rows=comp_count, row_step=0, out_dtype=jnp.float32,
    )
    return branch(
        queries, sel_kv, sel_lo, never, positions, gate_values[1], acc,
        sink=True, key_rows=TOPK * TILE, row_step=0, out_dtype=jnp.bfloat16, pick=pick,
    )


def solution(mesh):
    placed = (
        P("ctx", "head"),
        P(("ctx", "head"), None),
        P(("ctx", "head"), None),
        P(),
        P(),
        P(None, "head", "ctx"),
        P(),
    )

    return jax.shard_map(
        local, mesh=mesh, in_specs=placed, out_specs=P("ctx", "head"), check_vma=False
    )
```

```python
import functools

import jax
import jax.numpy as jnp
from jax import lax
from jax.experimental import pallas as pl
from jax.experimental.pallas import tpu as pltpu
from jax.sharding import PartitionSpec as P


H = 64
G = 4
HD = 128
KERN = 32
STRIDE = 16
TILE = 64
TOPK = 16
WIN = 512
QB = 256
CAP = 2
BIG = 1 << 30
CORES = 2


def shifted(block, axis, distance):
    devices = range(lax.axis_size(axis))
    route = [(i - distance, i) for i in devices if i - distance in devices]
    return lax.ppermute(block, axis, route)


def branch_kernel(*refs, sink, key_rows, row_step, heads, picks, with_acc):
    if picks:
        pick_ref, refs = refs[0], refs[1:]
        refs, pool_ref = refs[:-1], refs[-1]
    q_ref, kv_ref, lo_ref, hi_ref, t_ref, g_ref = refs[:6]
    if with_acc:
        acc_ref, o_ref = refs[6:]
    else:
        acc_ref = None
        (o_ref,) = refs[6:]
    block = pl.program_id(0)
    if picks:
        for k in range(picks):
            begin = pl.multiple_of(pick_ref[block, k] * TILE, TILE)
            pool_ref[k * TILE : (k + 1) * TILE, :] = kv_ref[pl.ds(begin, TILE), :]
        kv = pool_ref[...]
    elif row_step:
        start = pl.multiple_of(block * row_step, row_step)
        kv = kv_ref[pl.ds(start, key_rows), :]
    else:
        kv = kv_ref[...]
    keys = kv[:, :HD]
    vals = kv[:, HD:]
    lo = lo_ref[0]
    hi = hi_ref[0]
    t = t_ref[...]
    bias = jnp.where((lo <= t) & (t < hi), 0.0, -jnp.inf)
    for h in range(heads):
        q = q_ref[:, h * HD : (h + 1) * HD]
        s = lax.dot_general(
            q, keys, (((1,), (1,)), ((), ())), preferred_element_type=jnp.float32
        ) * HD ** (-0.5) + bias
        m = jnp.max(s, axis=1, keepdims=True)
        if sink:
            m = jnp.maximum(m, 0.0)
        p = jnp.exp(s - m)
        l = jnp.sum(p, axis=1, keepdims=True)
        if sink:
            l = l + jnp.exp(-m)
        o = jnp.dot(p.astype(jnp.bfloat16), vals, preferred_element_type=jnp.float32) / l
        r = g_ref[:, h : h + 1] * o
        if acc_ref is not None:
            r = acc_ref[:, h * HD : (h + 1) * HD] + r
        o_ref[:, h * HD : (h + 1) * HD] = r.astype(o_ref.dtype)


def branch(q, kv, lo, hi, t, gate, acc, *, sink, key_rows, row_step, out_dtype, pick=None):
    rows, width = q.shape
    heads = width // HD
    blocks = rows // QB
    lo_map = (lambda i, *_: (i, 0, 0)) if lo.shape[0] > 1 else (lambda i, *_: (0, 0, 0))
    hi_map = (lambda i, *_: (i, 0, 0)) if hi.shape[0] > 1 else (lambda i, *_: (0, 0, 0))
    row_map = lambda i, *_: (i, 0)
    in_specs = [
        pl.BlockSpec((QB, width), row_map),
        pl.BlockSpec(kv.shape, lambda i, *_: (0, 0)),
        pl.BlockSpec((1,) + lo.shape[1:], lo_map),
        pl.BlockSpec((1,) + hi.shape[1:], hi_map),
        pl.BlockSpec((QB, 1), row_map),
        pl.BlockSpec((QB, gate.shape[1]), row_map),
    ]
    args = [q, kv, lo, hi, t, gate]
    aliases = {}
    prefix = 0 if pick is None else 1
    if acc is not None:
        in_specs.append(pl.BlockSpec((QB, width), row_map))
        args.append(acc)
        if acc.dtype == out_dtype:
            aliases = {len(args) - 1 + prefix: 0}
    picks = 0 if pick is None else pick.shape[1]
    scratch = [] if pick is None else [pltpu.VMEM((key_rows, kv.shape[1]), kv.dtype)]
    kernel = functools.partial(
        branch_kernel, sink=sink, key_rows=key_rows, row_step=row_step, heads=heads,
        picks=picks, with_acc=acc is not None,
    )
    flops = 4 * rows * heads * key_rows * HD
    cost = pl.CostEstimate(
        flops=flops,
        transcendentals=rows * heads * key_rows,
        bytes_accessed=q.size * 2 + kv.size * 2 + rows * width * 8,
    )
    if pick is not None:
        args = [pick] + args
    return pl.pallas_call(
        kernel,
        grid_spec=pltpu.PrefetchScalarGridSpec(
            num_scalar_prefetch=prefix,
            grid=(blocks,),
            in_specs=in_specs,
            out_specs=pl.BlockSpec((QB, width), row_map),
            scratch_shapes=scratch,
        ),
        out_shape=jax.ShapeDtypeStruct((rows, width), out_dtype),
        input_output_aliases=aliases,
        compiler_params=pltpu.CompilerParams(
            dimension_semantics=("arbitrary",), vmem_limit_bytes=48 * 1024 * 1024
        ),
        cost_estimate=cost,
    )(*args)


def local(queries, keys, values, comp_k_weight, comp_v_weight, gate_logits, sel_tiles):
    ctx_count = lax.axis_size("ctx")
    head_count = lax.axis_size("head")
    ctx_index = lax.axis_index("ctx")
    head_index = lax.axis_index("head")
    local_rows = queries.shape[0]
    local_heads = queries.shape[1] // HD
    group_index = head_index * local_heads // (H // G)
    dev_rows = keys.shape[0]
    kv_rows = jnp.concatenate(
        [keys.reshape(dev_rows, G, HD), values.reshape(dev_rows, G, HD)], axis=2
    ).transpose(1, 0, 2)
    outbox_kv = jnp.repeat(kv_rows, (H // G) // local_heads, axis=0)
    group_kv = lax.all_to_all(outbox_kv, "head", 0, 0, tiled=True).reshape(
        local_rows, 2 * HD
    )
    tail_rows = shifted(group_kv[: KERN - STRIDE], "ctx", -1)
    extended = jnp.concatenate([group_kv, tail_rows], axis=0)
    comp_weight = jnp.concatenate(
        [
            lax.dynamic_slice_in_dim(comp_k_weight, group_index * HD, HD, 1),
            lax.dynamic_slice_in_dim(comp_v_weight, group_index * HD, HD, 1),
        ],
        axis=1,
    )
    comp_local = local_rows // STRIDE
    first_half = extended[:local_rows].reshape(comp_local, STRIDE, 2 * HD).astype(jnp.float32)
    second_half = (
        extended[STRIDE : STRIDE + local_rows]
        .reshape(comp_local, STRIDE, 2 * HD)
        .astype(jnp.float32)
    )
    compressed = (
        jnp.sum(first_half * comp_weight[None, :STRIDE], 1)
        + jnp.sum(second_half * comp_weight[None, STRIDE:], 1)
    ).astype(jnp.bfloat16)

    block_count = local_rows // QB
    tiles_shard = local_rows // TILE
    share = CORES
    part = head_index % share
    groups = [[g * share + i for i in range(share)] for g in range(head_count // share)]
    sel_share = CAP * TILE // share
    comp_share = comp_local // share
    group_tiles = lax.dynamic_slice_in_dim(sel_tiles, group_index * TOPK, TOPK, 1)
    own_tiles = lax.dynamic_slice_in_dim(group_tiles, ctx_index * block_count, block_count, 0)
    own_flat = own_tiles.reshape(-1)
    requests = group_tiles.reshape(ctx_count, block_count * TOPK)
    local_ids = ctx_index * tiles_shard + jnp.arange(tiles_shard)
    present = jnp.any(requests[:, :, None] == local_ids[None, None, :], axis=1)
    order_rank = jnp.cumsum(present.astype(jnp.int32), axis=1) - 1
    my_slot = part * sel_share // TILE
    my_row = part * sel_share % TILE
    picked = present & (order_rank == my_slot)
    tile_rows = lax.dynamic_slice_in_dim(
        group_kv.reshape(tiles_shard, TILE, 2 * HD), my_row, sel_share, 1
    )
    sel_part = jnp.einsum(
        "dt,tx->dx",
        picked.astype(jnp.bfloat16),
        tile_rows.reshape(tiles_shard, sel_share * 2 * HD),
        preferred_element_type=jnp.float32,
    ).astype(jnp.bfloat16).reshape(ctx_count, sel_share, 2 * HD)
    comp_part = jnp.broadcast_to(
        lax.dynamic_slice_in_dim(compressed, part * comp_share, comp_share, 0)[None],
        (ctx_count, comp_share, 2 * HD),
    )
    mail = jnp.concatenate([sel_part, comp_part], axis=1)
    arrived = lax.all_to_all(mail, "ctx", split_axis=0, concat_axis=0, tiled=True)
    spread = jnp.broadcast_to(arrived[None], (share,) + arrived.shape).reshape(
        (share * ctx_count,) + arrived.shape[1:]
    )
    gathered = lax.all_to_all(
        spread, "head", 0, 0, axis_index_groups=groups, tiled=True
    ).reshape((share,) + arrived.shape)
    sel_kv = gathered[:, :, :sel_share].reshape(share * ctx_count * sel_share, 2 * HD)
    comp_kv = gathered[:, :, sel_share:].reshape(share * ctx_count * comp_share, 2 * HD)
    comp_count = comp_kv.shape[0]
    all_ids = jnp.arange(ctx_count * tiles_shard).reshape(ctx_count, tiles_shard)
    wanted = jnp.any(own_flat[:, None, None] == all_ids[None, :, :], axis=0)
    wanted_rank = jnp.cumsum(wanted.astype(jnp.int32), axis=1) - 1
    chosen = wanted[:, None, :] & (wanted_rank[:, None, :] == jnp.arange(CAP)[None, :, None])
    slot_tile = jnp.sum(jnp.where(chosen, all_ids[:, None, :], 0), axis=2)
    slot_ok = jnp.any(chosen, axis=2)
    parts_per_slot = share // CAP
    row_in_tile = (
        jnp.arange(share)[:, None, None] % parts_per_slot * sel_share
        + jnp.arange(sel_share)[None, None, :]
    )
    key_tile = jnp.repeat(slot_tile, parts_per_slot, axis=1).T[:, :, None]
    key_pos = (key_tile * TILE + row_in_tile).reshape(-1)
    is_named = slot_ok[None] & jnp.any(
        own_tiles[:, :, None, None] == slot_tile[None, None], axis=1
    )
    key_named = jnp.broadcast_to(
        jnp.repeat(is_named, parts_per_slot, axis=2).transpose(0, 2, 1)[:, :, :, None],
        (block_count, share, ctx_count, sel_share),
    ).reshape(block_count, -1)
    slot_named = key_named.reshape(block_count, share * ctx_count, TILE)[:, :, 0]
    slot_base = key_pos.reshape(share * ctx_count, TILE)[:, 0]
    slot_rank = jnp.cumsum(slot_named.astype(jnp.int32), axis=1) - 1
    hit = slot_named[:, None, :] & (slot_rank[:, None, :] == jnp.arange(TOPK)[None, :, None])
    pick = jnp.sum(
        jnp.where(hit, jnp.arange(share * ctx_count)[None, None, :], 0), axis=2
    ).astype(jnp.int32)
    pick_base = jnp.sum(jnp.where(hit, slot_base[None, None, :], 0), axis=2)
    pick_ok = jnp.any(hit, axis=2)
    pick_pos = pick_base[:, :, None] + jnp.arange(TILE)[None, None, :]
    sel_lo = jnp.where(pick_ok[:, :, None], pick_pos, BIG).reshape(block_count, 1, TOPK * TILE)
    never = jnp.full((1, 1, TOPK * TILE), BIG, jnp.int32)

    comp_index = (
        jnp.arange(ctx_count)[None, :, None] * comp_local
        + jnp.arange(share)[:, None, None] * comp_share
        + jnp.arange(comp_share)[None, None, :]
    ).reshape(-1)
    comp_lo = (comp_index * STRIDE + KERN - 1).astype(jnp.int32).reshape(1, 1, comp_count)
    comp_hi = jnp.full((1, 1, comp_count), BIG, jnp.int32)

    win_rows = QB + WIN
    win_pos = (
        ctx_index * local_rows
        - WIN
        + jnp.arange(block_count)[:, None] * QB
        + jnp.arange(win_rows)[None, :]
    )
    win_lo = jnp.where(win_pos >= 0, win_pos, BIG).reshape(block_count, 1, win_rows)
    win_hi = (win_pos + WIN).reshape(block_count, 1, win_rows)

    positions = (ctx_index * local_rows + jnp.arange(local_rows, dtype=jnp.int32)).reshape(
        local_rows, 1
    )
    gate_values = jax.nn.sigmoid(gate_logits).transpose(0, 2, 1)

    previous = shifted(group_kv[local_rows - WIN :], "ctx", 1)
    window_kv = jnp.concatenate([previous, group_kv], axis=0)
    acc = branch(
        queries, window_kv, win_lo, win_hi, positions, gate_values[2], None,
        sink=False, key_rows=win_rows, row_step=QB, out_dtype=jnp.float32,
    )
    acc = branch(
        queries, comp_kv, comp_lo, comp_hi, positions, gate_values[0], acc,
        sink=True, key_rows=comp_count, row_step=0, out_dtype=jnp.float32,
    )
    return branch(
        queries, sel_kv, sel_lo, never, positions, gate_values[1], acc,
        sink=True, key_rows=TOPK * TILE, row_step=0, out_dtype=jnp.bfloat16, pick=pick,
    )


def solution(mesh):
    placed = (
        P("ctx", "head"),
        P(("ctx", "head"), None),
        P(("ctx", "head"), None),
        P(),
        P(),
        P(None, "head", "ctx"),
        P(),
    )

    return jax.shard_map(
        local, mesh=mesh, in_specs=placed, out_specs=P("ctx", "head"), check_vma=False
    )
```

```python
import functools

import jax
import jax.numpy as jnp
from jax import lax
from jax.experimental import pallas as pl
from jax.experimental.pallas import tpu as pltpu
from jax.sharding import PartitionSpec as P


H = 64
G = 4
HD = 128
KERN = 32
STRIDE = 16
TILE = 64
TOPK = 16
WIN = 512
QB = 256
CAP = 2
BIG = 1 << 30
CORES = 2


def shifted(block, axis, distance):
    devices = range(lax.axis_size(axis))
    route = [(i - distance, i) for i in devices if i - distance in devices]
    return lax.ppermute(block, axis, route)


def branch_kernel(*refs, sink, key_rows, row_step, heads, picks, with_acc):
    if picks:
        pick_ref, refs = refs[0], refs[1:]
        refs, pool_ref = refs[:-1], refs[-1]
    q_ref, kv_ref, lo_ref, hi_ref, t_ref, g_ref = refs[:6]
    if with_acc:
        acc_ref, o_ref = refs[6:]
    else:
        acc_ref = None
        (o_ref,) = refs[6:]
    block = pl.program_id(0)
    if picks:
        for k in range(picks):
            begin = pl.multiple_of(pick_ref[block, k] * TILE, TILE)
            pool_ref[k * TILE : (k + 1) * TILE, :] = kv_ref[pl.ds(begin, TILE), :]
        kv = pool_ref[...]
    elif row_step:
        start = pl.multiple_of(block * row_step, row_step)
        kv = kv_ref[pl.ds(start, key_rows), :]
    else:
        kv = kv_ref[...]
    keys = kv[:, :HD]
    vals = kv[:, HD:]
    lo = lo_ref[0]
    hi = hi_ref[0]
    t = t_ref[...]
    bias = jnp.where((lo <= t) & (t < hi), 0.0, -jnp.inf)
    for h in range(heads):
        q = q_ref[:, h * HD : (h + 1) * HD]
        s = lax.dot_general(
            q, keys, (((1,), (1,)), ((), ())), preferred_element_type=jnp.float32
        ) * HD ** (-0.5) + bias
        m = jnp.max(s, axis=1, keepdims=True)
        if sink:
            m = jnp.maximum(m, 0.0)
        p = jnp.exp(s - m)
        l = jnp.sum(p, axis=1, keepdims=True)
        if sink:
            l = l + jnp.exp(-m)
        o = jnp.dot(p.astype(jnp.bfloat16), vals, preferred_element_type=jnp.float32) / l
        r = g_ref[:, h : h + 1] * o
        if acc_ref is not None:
            r = acc_ref[:, h * HD : (h + 1) * HD] + r
        o_ref[:, h * HD : (h + 1) * HD] = r.astype(o_ref.dtype)


def branch(q, kv, lo, hi, t, gate, acc, *, sink, key_rows, row_step, out_dtype, pick=None):
    rows, width = q.shape
    heads = width // HD
    blocks = rows // QB
    lo_map = (lambda i, *_: (i, 0, 0)) if lo.shape[0] > 1 else (lambda i, *_: (0, 0, 0))
    hi_map = (lambda i, *_: (i, 0, 0)) if hi.shape[0] > 1 else (lambda i, *_: (0, 0, 0))
    row_map = lambda i, *_: (i, 0)
    in_specs = [
        pl.BlockSpec((QB, width), row_map),
        pl.BlockSpec(kv.shape, lambda i, *_: (0, 0)),
        pl.BlockSpec((1,) + lo.shape[1:], lo_map),
        pl.BlockSpec((1,) + hi.shape[1:], hi_map),
        pl.BlockSpec((QB, 1), row_map),
        pl.BlockSpec((QB, gate.shape[1]), row_map),
    ]
    args = [q, kv, lo, hi, t, gate]
    aliases = {}
    prefix = 0 if pick is None else 1
    if acc is not None:
        in_specs.append(pl.BlockSpec((QB, width), row_map))
        args.append(acc)
        if acc.dtype == out_dtype:
            aliases = {len(args) - 1 + prefix: 0}
    picks = 0 if pick is None else pick.shape[1]
    scratch = [] if pick is None else [pltpu.VMEM((key_rows, kv.shape[1]), kv.dtype)]
    kernel = functools.partial(
        branch_kernel, sink=sink, key_rows=key_rows, row_step=row_step, heads=heads,
        picks=picks, with_acc=acc is not None,
    )
    flops = 4 * rows * heads * key_rows * HD
    cost = pl.CostEstimate(
        flops=flops,
        transcendentals=rows * heads * key_rows,
        bytes_accessed=q.size * 2 + kv.size * 2 + rows * width * 8,
    )
    if pick is not None:
        args = [pick] + args
    return pl.pallas_call(
        kernel,
        grid_spec=pltpu.PrefetchScalarGridSpec(
            num_scalar_prefetch=prefix,
            grid=(blocks,),
            in_specs=in_specs,
            out_specs=pl.BlockSpec((QB, width), row_map),
            scratch_shapes=scratch,
        ),
        out_shape=jax.ShapeDtypeStruct((rows, width), out_dtype),
        input_output_aliases=aliases,
        compiler_params=pltpu.CompilerParams(
            dimension_semantics=("arbitrary",), vmem_limit_bytes=48 * 1024 * 1024
        ),
        cost_estimate=cost,
    )(*args)


def sink_attend(q, keys, vals, bias):
    s = lax.dot_general(
        q, keys, (((1,), (1,)), ((), ())), preferred_element_type=jnp.float32
    ) * HD ** (-0.5) + bias
    m = jnp.maximum(jnp.max(s, axis=1, keepdims=True), 0.0)
    p = jnp.exp(s - m)
    l = jnp.sum(p, axis=1, keepdims=True) + jnp.exp(-m)
    return jnp.dot(p.astype(jnp.bfloat16), vals, preferred_element_type=jnp.float32) / l


def late_kernel(pick_ref, q_ref, ckv_ref, clo_ref, skv_ref, slo_ref, t_ref, gc_ref, gs_ref,
                acc_ref, o_ref, pool_ref, *, heads, picks):
    block = pl.program_id(0)
    for k in range(picks):
        begin = pl.multiple_of(pick_ref[block, k] * TILE, TILE)
        pool_ref[k * TILE : (k + 1) * TILE, :] = skv_ref[pl.ds(begin, TILE), :]
    t = t_ref[...]
    comp_bias = jnp.where(clo_ref[0] <= t, 0.0, -jnp.inf)
    sel_bias = jnp.where(slo_ref[0] <= t, 0.0, -jnp.inf)
    ckv = ckv_ref[...]
    skv = pool_ref[...]
    for h in range(heads):
        q = q_ref[:, h * HD : (h + 1) * HD]
        oc = sink_attend(q, ckv[:, :HD], ckv[:, HD:], comp_bias)
        osel = sink_attend(q, skv[:, :HD], skv[:, HD:], sel_bias)
        r = acc_ref[:, h * HD : (h + 1) * HD] + gc_ref[:, h : h + 1] * oc
        r = r + gs_ref[:, h : h + 1] * osel
        o_ref[:, h * HD : (h + 1) * HD] = r.astype(o_ref.dtype)


def late_branches(q, ckv, clo, skv, slo, pick, t, gate_c, gate_s, acc):
    rows, width = q.shape
    heads = width // HD
    blocks = rows // QB
    picks = pick.shape[1]
    sel_keys = picks * TILE
    row_map = lambda i, *_: (i, 0)
    whole = lambda i, *_: (0, 0)
    in_specs = [
        pl.BlockSpec((QB, width), row_map),
        pl.BlockSpec(ckv.shape, whole),
        pl.BlockSpec((1,) + clo.shape[1:], lambda i, *_: (0, 0, 0)),
        pl.BlockSpec(skv.shape, whole),
        pl.BlockSpec((1,) + slo.shape[1:], lambda i, *_: (i, 0, 0)),
        pl.BlockSpec((QB, 1), row_map),
        pl.BlockSpec((QB, gate_c.shape[1]), row_map),
        pl.BlockSpec((QB, gate_s.shape[1]), row_map),
        pl.BlockSpec((QB, width), row_map),
    ]
    key_rows = ckv.shape[0] + sel_keys
    cost = pl.CostEstimate(
        flops=4 * rows * heads * key_rows * HD,
        transcendentals=rows * heads * key_rows,
        bytes_accessed=q.size * 2 + ckv.size * 2 + skv.size * 2 + rows * width * 6,
    )
    return pl.pallas_call(
        functools.partial(late_kernel, heads=heads, picks=picks),
        grid_spec=pltpu.PrefetchScalarGridSpec(
            num_scalar_prefetch=1,
            grid=(blocks,),
            in_specs=in_specs,
            out_specs=pl.BlockSpec((QB, width), row_map),
            scratch_shapes=[pltpu.VMEM((sel_keys, skv.shape[1]), skv.dtype)],
        ),
        out_shape=jax.ShapeDtypeStruct((rows, width), jnp.bfloat16),
        compiler_params=pltpu.CompilerParams(
            dimension_semantics=("arbitrary",), vmem_limit_bytes=48 * 1024 * 1024
        ),
        cost_estimate=cost,
    )(pick, q, ckv, clo, skv, slo, t, gate_c, gate_s, acc)


def local(queries, keys, values, comp_k_weight, comp_v_weight, gate_logits, sel_tiles):
    ctx_count = lax.axis_size("ctx")
    head_count = lax.axis_size("head")
    ctx_index = lax.axis_index("ctx")
    head_index = lax.axis_index("head")
    local_rows = queries.shape[0]
    local_heads = queries.shape[1] // HD
    group_index = head_index * local_heads // (H // G)
    dev_rows = keys.shape[0]
    kv_rows = jnp.concatenate(
        [keys.reshape(dev_rows, G, HD), values.reshape(dev_rows, G, HD)], axis=2
    ).transpose(1, 0, 2)
    outbox_kv = jnp.repeat(kv_rows, (H // G) // local_heads, axis=0)
    group_kv = lax.all_to_all(outbox_kv, "head", 0, 0, tiled=True).reshape(
        local_rows, 2 * HD
    )
    previous = shifted(group_kv[local_rows - WIN :], "ctx", 1)
    window_kv = jnp.concatenate([previous, group_kv], axis=0)
    extended = window_kv[WIN - STRIDE :]
    comp_weight = jnp.concatenate(
        [
            lax.dynamic_slice_in_dim(comp_k_weight, group_index * HD, HD, 1),
            lax.dynamic_slice_in_dim(comp_v_weight, group_index * HD, HD, 1),
        ],
        axis=1,
    )
    comp_local = local_rows // STRIDE
    first_half = extended[:local_rows].reshape(comp_local, STRIDE, 2 * HD).astype(jnp.float32)
    second_half = (
        extended[STRIDE : STRIDE + local_rows]
        .reshape(comp_local, STRIDE, 2 * HD)
        .astype(jnp.float32)
    )
    compressed = (
        jnp.sum(first_half * comp_weight[None, :STRIDE], 1)
        + jnp.sum(second_half * comp_weight[None, STRIDE:], 1)
    ).astype(jnp.bfloat16)

    block_count = local_rows // QB
    tiles_shard = local_rows // TILE
    share = CORES
    part = head_index % share
    groups = [[g * share + i for i in range(share)] for g in range(head_count // share)]
    sel_share = CAP * TILE // share
    comp_share = comp_local // share
    group_tiles = lax.dynamic_slice_in_dim(sel_tiles, group_index * TOPK, TOPK, 1)
    own_tiles = lax.dynamic_slice_in_dim(group_tiles, ctx_index * block_count, block_count, 0)
    own_flat = own_tiles.reshape(-1)
    requests = group_tiles.reshape(ctx_count, block_count * TOPK)
    local_ids = ctx_index * tiles_shard + jnp.arange(tiles_shard)
    present = jnp.any(requests[:, :, None] == local_ids[None, None, :], axis=1)
    order_rank = jnp.cumsum(present.astype(jnp.int32), axis=1) - 1
    my_slot = part * sel_share // TILE
    my_row = part * sel_share % TILE
    picked = present & (order_rank == my_slot)
    tile_rows = lax.dynamic_slice_in_dim(
        group_kv.reshape(tiles_shard, TILE, 2 * HD), my_row, sel_share, 1
    )
    sel_part = jnp.einsum(
        "dt,tx->dx",
        picked.astype(jnp.bfloat16),
        tile_rows.reshape(tiles_shard, sel_share * 2 * HD),
        preferred_element_type=jnp.float32,
    ).astype(jnp.bfloat16).reshape(ctx_count, sel_share, 2 * HD)
    comp_part = jnp.broadcast_to(
        lax.dynamic_slice_in_dim(compressed, part * comp_share, comp_share, 0)[None],
        (ctx_count, comp_share, 2 * HD),
    )
    mail = jnp.concatenate([sel_part, comp_part], axis=1)
    arrived = lax.all_to_all(mail, "ctx", split_axis=0, concat_axis=0, tiled=True)
    spread = jnp.broadcast_to(arrived[None], (share,) + arrived.shape).reshape(
        (share * ctx_count,) + arrived.shape[1:]
    )
    gathered = lax.all_to_all(
        spread, "head", 0, 0, axis_index_groups=groups, tiled=True
    ).reshape((share,) + arrived.shape)
    sel_kv = gathered[:, :, :sel_share].reshape(share * ctx_count * sel_share, 2 * HD)
    comp_kv = gathered[:, :, sel_share:].reshape(share * ctx_count * comp_share, 2 * HD)
    comp_count = comp_kv.shape[0]
    all_ids = jnp.arange(ctx_count * tiles_shard).reshape(ctx_count, tiles_shard)
    wanted = jnp.any(own_flat[:, None, None] == all_ids[None, :, :], axis=0)
    wanted_rank = jnp.cumsum(wanted.astype(jnp.int32), axis=1) - 1
    chosen = wanted[:, None, :] & (wanted_rank[:, None, :] == jnp.arange(CAP)[None, :, None])
    slot_tile = jnp.sum(jnp.where(chosen, all_ids[:, None, :], 0), axis=2)
    slot_ok = jnp.any(chosen, axis=2)
    parts_per_slot = share // CAP
    row_in_tile = (
        jnp.arange(share)[:, None, None] % parts_per_slot * sel_share
        + jnp.arange(sel_share)[None, None, :]
    )
    key_tile = jnp.repeat(slot_tile, parts_per_slot, axis=1).T[:, :, None]
    key_pos = (key_tile * TILE + row_in_tile).reshape(-1)
    is_named = slot_ok[None] & jnp.any(
        own_tiles[:, :, None, None] == slot_tile[None, None], axis=1
    )
    key_named = jnp.broadcast_to(
        jnp.repeat(is_named, parts_per_slot, axis=2).transpose(0, 2, 1)[:, :, :, None],
        (block_count, share, ctx_count, sel_share),
    ).reshape(block_count, -1)
    slot_named = key_named.reshape(block_count, share * ctx_count, TILE)[:, :, 0]
    slot_base = key_pos.reshape(share * ctx_count, TILE)[:, 0]
    slot_rank = jnp.cumsum(slot_named.astype(jnp.int32), axis=1) - 1
    hit = slot_named[:, None, :] & (slot_rank[:, None, :] == jnp.arange(TOPK)[None, :, None])
    pick = jnp.sum(
        jnp.where(hit, jnp.arange(share * ctx_count)[None, None, :], 0), axis=2
    ).astype(jnp.int32)
    pick_base = jnp.sum(jnp.where(hit, slot_base[None, None, :], 0), axis=2)
    pick_ok = jnp.any(hit, axis=2)
    pick_pos = pick_base[:, :, None] + jnp.arange(TILE)[None, None, :]
    sel_lo = jnp.where(pick_ok[:, :, None], pick_pos, BIG).reshape(block_count, 1, TOPK * TILE)
    never = jnp.full((1, 1, TOPK * TILE), BIG, jnp.int32)

    comp_index = (
        jnp.arange(ctx_count)[None, :, None] * comp_local
        + jnp.arange(share)[:, None, None] * comp_share
        + jnp.arange(comp_share)[None, None, :]
    ).reshape(-1)
    comp_block = comp_index - 1
    comp_lo = jnp.where(comp_block >= 0, comp_block * STRIDE + KERN - 1, BIG)
    comp_lo = comp_lo.astype(jnp.int32).reshape(1, 1, comp_count)
    comp_hi = jnp.full((1, 1, comp_count), BIG, jnp.int32)

    win_rows = QB + WIN
    win_pos = (
        ctx_index * local_rows
        - WIN
        + jnp.arange(block_count)[:, None] * QB
        + jnp.arange(win_rows)[None, :]
    )
    win_lo = jnp.where(win_pos >= 0, win_pos, BIG).reshape(block_count, 1, win_rows)
    win_hi = (win_pos + WIN).reshape(block_count, 1, win_rows)

    positions = (ctx_index * local_rows + jnp.arange(local_rows, dtype=jnp.int32)).reshape(
        local_rows, 1
    )
    gate_values = jax.nn.sigmoid(gate_logits).transpose(0, 2, 1)

    acc = branch(
        queries, window_kv, win_lo, win_hi, positions, gate_values[2], None,
        sink=False, key_rows=win_rows, row_step=QB, out_dtype=jnp.float32,
    )
    return late_branches(
        queries, comp_kv, comp_lo, sel_kv, sel_lo, pick, positions,
        gate_values[0], gate_values[1], acc,
    )


def solution(mesh):
    placed = (
        P("ctx", "head"),
        P(("ctx", "head"), None),
        P(("ctx", "head"), None),
        P(),
        P(),
        P(None, "head", "ctx"),
        P(),
    )

    return jax.shard_map(
        local, mesh=mesh, in_specs=placed, out_specs=P("ctx", "head"), check_vma=False
    )
```

```python
import functools

import jax
import jax.numpy as jnp
from jax import lax
from jax.experimental import pallas as pl
from jax.experimental.pallas import tpu as pltpu
from jax.sharding import PartitionSpec as P


H = 64
G = 4
HD = 128
KERN = 32
STRIDE = 16
TILE = 64
TOPK = 16
WIN = 512
QB = 256
CAP = 2
BIG = 1 << 30
CORES = 2


def shifted(block, axis, distance):
    devices = range(lax.axis_size(axis))
    route = [(i - distance, i) for i in devices if i - distance in devices]
    return lax.ppermute(block, axis, route)


def branch_kernel(*refs, sink, key_rows, row_step, heads, picks, with_acc):
    if picks:
        pick_ref, refs = refs[0], refs[1:]
        refs, pool_ref = refs[:-1], refs[-1]
    q_ref, kv_ref, lo_ref, hi_ref, t_ref, g_ref = refs[:6]
    if with_acc:
        acc_ref, o_ref = refs[6:]
    else:
        acc_ref = None
        (o_ref,) = refs[6:]
    block = pl.program_id(0)
    if picks:
        for k in range(picks):
            begin = pl.multiple_of(pick_ref[block, k] * TILE, TILE)
            pool_ref[k * TILE : (k + 1) * TILE, :] = kv_ref[pl.ds(begin, TILE), :]
        kv = pool_ref[...]
    elif row_step:
        start = pl.multiple_of(block * row_step, row_step)
        kv = kv_ref[pl.ds(start, key_rows), :]
    else:
        kv = kv_ref[...]
    keys = kv[:, :HD]
    vals = kv[:, HD:]
    lo = lo_ref[0]
    hi = hi_ref[0]
    t = t_ref[...]
    bias = jnp.where((lo <= t) & (t < hi), 0.0, -jnp.inf)
    for h in range(heads):
        q = q_ref[:, h * HD : (h + 1) * HD]
        s = lax.dot_general(
            q, keys, (((1,), (1,)), ((), ())), preferred_element_type=jnp.float32
        ) * HD ** (-0.5) + bias
        m = jnp.max(s, axis=1, keepdims=True)
        if sink:
            m = jnp.maximum(m, 0.0)
        p = jnp.exp(s - m)
        l = jnp.sum(p, axis=1, keepdims=True)
        if sink:
            l = l + jnp.exp(-m)
        o = jnp.dot(p.astype(jnp.bfloat16), vals, preferred_element_type=jnp.float32) / l
        r = g_ref[:, h : h + 1] * o
        if acc_ref is not None:
            r = acc_ref[:, h * HD : (h + 1) * HD] + r
        o_ref[:, h * HD : (h + 1) * HD] = r.astype(o_ref.dtype)


def branch(q, kv, lo, hi, t, gate, acc, *, sink, key_rows, row_step, out_dtype, pick=None):
    rows, width = q.shape
    heads = width // HD
    blocks = rows // QB
    lo_map = (lambda i, *_: (i, 0, 0)) if lo.shape[0] > 1 else (lambda i, *_: (0, 0, 0))
    hi_map = (lambda i, *_: (i, 0, 0)) if hi.shape[0] > 1 else (lambda i, *_: (0, 0, 0))
    row_map = lambda i, *_: (i, 0)
    in_specs = [
        pl.BlockSpec((QB, width), row_map),
        pl.BlockSpec(kv.shape, lambda i, *_: (0, 0)),
        pl.BlockSpec((1,) + lo.shape[1:], lo_map),
        pl.BlockSpec((1,) + hi.shape[1:], hi_map),
        pl.BlockSpec((QB, 1), row_map),
        pl.BlockSpec((QB, gate.shape[1]), row_map),
    ]
    args = [q, kv, lo, hi, t, gate]
    aliases = {}
    prefix = 0 if pick is None else 1
    if acc is not None:
        in_specs.append(pl.BlockSpec((QB, width), row_map))
        args.append(acc)
        if acc.dtype == out_dtype:
            aliases = {len(args) - 1 + prefix: 0}
    picks = 0 if pick is None else pick.shape[1]
    scratch = [] if pick is None else [pltpu.VMEM((key_rows, kv.shape[1]), kv.dtype)]
    kernel = functools.partial(
        branch_kernel, sink=sink, key_rows=key_rows, row_step=row_step, heads=heads,
        picks=picks, with_acc=acc is not None,
    )
    flops = 4 * rows * heads * key_rows * HD
    cost = pl.CostEstimate(
        flops=flops,
        transcendentals=rows * heads * key_rows,
        bytes_accessed=q.size * 2 + kv.size * 2 + rows * width * 8,
    )
    if pick is not None:
        args = [pick] + args
    return pl.pallas_call(
        kernel,
        grid_spec=pltpu.PrefetchScalarGridSpec(
            num_scalar_prefetch=prefix,
            grid=(blocks,),
            in_specs=in_specs,
            out_specs=pl.BlockSpec((QB, width), row_map),
            scratch_shapes=scratch,
        ),
        out_shape=jax.ShapeDtypeStruct((rows, width), out_dtype),
        input_output_aliases=aliases,
        compiler_params=pltpu.CompilerParams(
            dimension_semantics=("arbitrary",), vmem_limit_bytes=48 * 1024 * 1024
        ),
        cost_estimate=cost,
    )(*args)


def sink_attend(q, keys, vals, bias):
    s = lax.dot_general(
        q, keys, (((1,), (1,)), ((), ())), preferred_element_type=jnp.float32
    ) * HD ** (-0.5) + bias
    m = jnp.maximum(jnp.max(s, axis=1, keepdims=True), 0.0)
    p = jnp.exp(s - m)
    l = jnp.sum(p, axis=1, keepdims=True) + jnp.exp(-m)
    return jnp.dot(p.astype(jnp.bfloat16), vals, preferred_element_type=jnp.float32) / l


def late_kernel(pick_ref, q_ref, ckv_ref, clo_ref, skv_ref, slo_ref, t_ref, gc_ref, gs_ref,
                acc_ref, o_ref, pool_ref, *, heads, picks):
    block = pl.program_id(0)
    for k in range(picks):
        begin = pl.multiple_of(pick_ref[block, k] * TILE, TILE)
        pool_ref[k * TILE : (k + 1) * TILE, :] = skv_ref[pl.ds(begin, TILE), :]
    t = t_ref[...]
    comp_bias = jnp.where(clo_ref[0] <= t, 0.0, -jnp.inf)
    sel_bias = jnp.where(slo_ref[0] <= t, 0.0, -jnp.inf)
    ckv = ckv_ref[...]
    skv = pool_ref[...]
    for h in range(heads):
        q = q_ref[:, h * HD : (h + 1) * HD]
        oc = sink_attend(q, ckv[:, :HD], ckv[:, HD:], comp_bias)
        osel = sink_attend(q, skv[:, :HD], skv[:, HD:], sel_bias)
        r = acc_ref[:, h * HD : (h + 1) * HD] + gc_ref[:, h : h + 1] * oc
        r = r + gs_ref[:, h : h + 1] * osel
        o_ref[:, h * HD : (h + 1) * HD] = r.astype(o_ref.dtype)


def late_branches(q, ckv, clo, skv, slo, pick, t, gate_c, gate_s, acc):
    rows, width = q.shape
    heads = width // HD
    blocks = rows // QB
    picks = pick.shape[1]
    sel_keys = picks * TILE
    row_map = lambda i, *_: (i, 0)
    whole = lambda i, *_: (0, 0)
    in_specs = [
        pl.BlockSpec((QB, width), row_map),
        pl.BlockSpec(ckv.shape, whole),
        pl.BlockSpec((1,) + clo.shape[1:], lambda i, *_: (0, 0, 0)),
        pl.BlockSpec(skv.shape, whole),
        pl.BlockSpec((1,) + slo.shape[1:], lambda i, *_: (i, 0, 0)),
        pl.BlockSpec((QB, 1), row_map),
        pl.BlockSpec((QB, gate_c.shape[1]), row_map),
        pl.BlockSpec((QB, gate_s.shape[1]), row_map),
        pl.BlockSpec((QB, width), row_map),
    ]
    key_rows = ckv.shape[0] + sel_keys
    cost = pl.CostEstimate(
        flops=4 * rows * heads * key_rows * HD,
        transcendentals=rows * heads * key_rows,
        bytes_accessed=q.size * 2 + ckv.size * 2 + skv.size * 2 + rows * width * 6,
    )
    return pl.pallas_call(
        functools.partial(late_kernel, heads=heads, picks=picks),
        grid_spec=pltpu.PrefetchScalarGridSpec(
            num_scalar_prefetch=1,
            grid=(blocks,),
            in_specs=in_specs,
            out_specs=pl.BlockSpec((QB, width), row_map),
            scratch_shapes=[pltpu.VMEM((sel_keys, skv.shape[1]), skv.dtype)],
        ),
        out_shape=jax.ShapeDtypeStruct((rows, width), jnp.bfloat16),
        compiler_params=pltpu.CompilerParams(
            dimension_semantics=("arbitrary",), vmem_limit_bytes=48 * 1024 * 1024
        ),
        cost_estimate=cost,
    )(pick, q, ckv, clo, skv, slo, t, gate_c, gate_s, acc)


def local(queries, keys, values, comp_k_weight, comp_v_weight, gate_logits, sel_tiles):
    ctx_count = lax.axis_size("ctx")
    head_count = lax.axis_size("head")
    ctx_index = lax.axis_index("ctx")
    head_index = lax.axis_index("head")
    local_rows = queries.shape[0]
    local_heads = queries.shape[1] // HD
    group_index = head_index * local_heads // (H // G)
    dev_rows = keys.shape[0]
    kv_rows = jnp.concatenate(
        [keys.reshape(dev_rows, G, HD), values.reshape(dev_rows, G, HD)], axis=2
    ).transpose(1, 0, 2)
    outbox_kv = jnp.repeat(kv_rows, (H // G) // local_heads, axis=0)
    group_kv = lax.all_to_all(outbox_kv, "head", 0, 0, tiled=True).reshape(
        local_rows, 2 * HD
    )
    previous = shifted(group_kv[local_rows - WIN :], "ctx", 1)
    window_kv = jnp.concatenate([previous, group_kv], axis=0)
    extended = window_kv[WIN - STRIDE :]
    comp_weight = jnp.concatenate(
        [
            lax.dynamic_slice_in_dim(comp_k_weight, group_index * HD, HD, 1),
            lax.dynamic_slice_in_dim(comp_v_weight, group_index * HD, HD, 1),
        ],
        axis=1,
    )
    comp_local = local_rows // STRIDE
    first_half = extended[:local_rows].reshape(comp_local, STRIDE, 2 * HD).astype(jnp.float32)
    second_half = (
        extended[STRIDE : STRIDE + local_rows]
        .reshape(comp_local, STRIDE, 2 * HD)
        .astype(jnp.float32)
    )
    compressed = (
        jnp.sum(first_half * comp_weight[None, :STRIDE], 1)
        + jnp.sum(second_half * comp_weight[None, STRIDE:], 1)
    ).astype(jnp.bfloat16)

    block_count = local_rows // QB
    tiles_shard = local_rows // TILE
    share = CORES
    part = head_index % share
    sel_share = CAP * TILE // share
    comp_share = comp_local // share
    group_tiles = lax.dynamic_slice_in_dim(sel_tiles, group_index * TOPK, TOPK, 1)
    own_tiles = lax.dynamic_slice_in_dim(group_tiles, ctx_index * block_count, block_count, 0)
    own_flat = own_tiles.reshape(-1)
    requests = group_tiles.reshape(ctx_count, block_count * TOPK)
    local_ids = ctx_index * tiles_shard + jnp.arange(tiles_shard)
    present = jnp.any(requests[:, :, None] == local_ids[None, None, :], axis=1)
    order_rank = jnp.cumsum(present.astype(jnp.int32), axis=1) - 1
    my_slot = part * sel_share // TILE
    my_row = part * sel_share % TILE
    picked = present & (order_rank == my_slot)
    tile_rows = lax.dynamic_slice_in_dim(
        group_kv.reshape(tiles_shard, TILE, 2 * HD), my_row, sel_share, 1
    )
    sel_part = jnp.einsum(
        "dt,tx->dx",
        picked.astype(jnp.bfloat16),
        tile_rows.reshape(tiles_shard, sel_share * 2 * HD),
        preferred_element_type=jnp.float32,
    ).astype(jnp.bfloat16).reshape(ctx_count, sel_share, 2 * HD)
    comp_part = jnp.broadcast_to(
        lax.dynamic_slice_in_dim(compressed, part * comp_share, comp_share, 0)[None],
        (ctx_count, comp_share, 2 * HD),
    )
    mail = jnp.concatenate([sel_part, comp_part], axis=1)
    arrived = lax.all_to_all(mail, "ctx", split_axis=0, concat_axis=0, tiled=True)
    partner = lax.ppermute(arrived, "head", [(i, i ^ 1) for i in range(head_count)])
    gathered = jnp.where(
        part == 0, jnp.stack([arrived, partner]), jnp.stack([partner, arrived])
    )
    sel_kv = gathered[:, :, :sel_share].reshape(share * ctx_count * sel_share, 2 * HD)
    comp_kv = gathered[:, :, sel_share:].reshape(share * ctx_count * comp_share, 2 * HD)
    comp_count = comp_kv.shape[0]
    all_ids = jnp.arange(ctx_count * tiles_shard).reshape(ctx_count, tiles_shard)
    wanted = jnp.any(own_flat[:, None, None] == all_ids[None, :, :], axis=0)
    wanted_rank = jnp.cumsum(wanted.astype(jnp.int32), axis=1) - 1
    chosen = wanted[:, None, :] & (wanted_rank[:, None, :] == jnp.arange(CAP)[None, :, None])
    slot_tile = jnp.sum(jnp.where(chosen, all_ids[:, None, :], 0), axis=2)
    slot_ok = jnp.any(chosen, axis=2)
    parts_per_slot = share // CAP
    row_in_tile = (
        jnp.arange(share)[:, None, None] % parts_per_slot * sel_share
        + jnp.arange(sel_share)[None, None, :]
    )
    key_tile = jnp.repeat(slot_tile, parts_per_slot, axis=1).T[:, :, None]
    key_pos = (key_tile * TILE + row_in_tile).reshape(-1)
    is_named = slot_ok[None] & jnp.any(
        own_tiles[:, :, None, None] == slot_tile[None, None], axis=1
    )
    key_named = jnp.broadcast_to(
        jnp.repeat(is_named, parts_per_slot, axis=2).transpose(0, 2, 1)[:, :, :, None],
        (block_count, share, ctx_count, sel_share),
    ).reshape(block_count, -1)
    slot_named = key_named.reshape(block_count, share * ctx_count, TILE)[:, :, 0]
    slot_base = key_pos.reshape(share * ctx_count, TILE)[:, 0]
    slot_rank = jnp.cumsum(slot_named.astype(jnp.int32), axis=1) - 1
    hit = slot_named[:, None, :] & (slot_rank[:, None, :] == jnp.arange(TOPK)[None, :, None])
    pick = jnp.sum(
        jnp.where(hit, jnp.arange(share * ctx_count)[None, None, :], 0), axis=2
    ).astype(jnp.int32)
    pick_base = jnp.sum(jnp.where(hit, slot_base[None, None, :], 0), axis=2)
    pick_ok = jnp.any(hit, axis=2)
    pick_pos = pick_base[:, :, None] + jnp.arange(TILE)[None, None, :]
    sel_lo = jnp.where(pick_ok[:, :, None], pick_pos, BIG).reshape(block_count, 1, TOPK * TILE)
    never = jnp.full((1, 1, TOPK * TILE), BIG, jnp.int32)

    comp_index = (
        jnp.arange(ctx_count)[None, :, None] * comp_local
        + jnp.arange(share)[:, None, None] * comp_share
        + jnp.arange(comp_share)[None, None, :]
    ).reshape(-1)
    comp_block = comp_index - 1
    comp_lo = jnp.where(comp_block >= 0, comp_block * STRIDE + KERN - 1, BIG)
    comp_lo = comp_lo.astype(jnp.int32).reshape(1, 1, comp_count)
    comp_hi = jnp.full((1, 1, comp_count), BIG, jnp.int32)

    win_rows = QB + WIN
    win_pos = (
        ctx_index * local_rows
        - WIN
        + jnp.arange(block_count)[:, None] * QB
        + jnp.arange(win_rows)[None, :]
    )
    win_lo = jnp.where(win_pos >= 0, win_pos, BIG).reshape(block_count, 1, win_rows)
    win_hi = (win_pos + WIN).reshape(block_count, 1, win_rows)

    positions = (ctx_index * local_rows + jnp.arange(local_rows, dtype=jnp.int32)).reshape(
        local_rows, 1
    )
    gate_values = jax.nn.sigmoid(gate_logits).transpose(0, 2, 1)

    acc = branch(
        queries, window_kv, win_lo, win_hi, positions, gate_values[2], None,
        sink=False, key_rows=win_rows, row_step=QB, out_dtype=jnp.float32,
    )
    return late_branches(
        queries, comp_kv, comp_lo, sel_kv, sel_lo, pick, positions,
        gate_values[0], gate_values[1], acc,
    )


def solution(mesh):
    placed = (
        P("ctx", "head"),
        P(("ctx", "head"), None),
        P(("ctx", "head"), None),
        P(),
        P(),
        P(None, "head", "ctx"),
        P(),
    )

    return jax.shard_map(
        local, mesh=mesh, in_specs=placed, out_specs=P("ctx", "head"), check_vma=False
    )
```
